32 devices in a mesh: tm: 16 (over z, y, x), rows: 2 (over core).
Axes of the slice: x: 2, y: 2, z: 4, core: 2. Of those that a mesh axis runs over, the one named last changes fastest.
Arguments:
- observed: float32 [192, 512, 128], P('tm', 'rows'), may hold values from -12 to 12
- gain: float32 [192, 512], P('tm'), may hold values from 2.5e-05 to 0.525
- smooth_gain: float32 [192, 512], P('tm'), may hold values from 0.475 to 0.999975
- dynamics: float32 [512, 512], replicated, may hold values from -0.0021213203 to 0.9998
- pattern: int32 [8, 8], replicated, may hold values from 0 to 1, as said below
- initial: float32 [512, 128], P('rows'), may hold values from -6 to 6
- lengths: int32 [16], P('tm'), may hold values from 1 to 12, 144 in all
Outputs:
- filtered: float32 [192, 512, 128], P('tm', 'rows')
- smoothed: float32 [192, 512, 128], P('tm', 'rows')
The draws below stay inside these ranges and needn't reach their ends.
Inputs may be any that keep to these rules, and one draw needn't show every extreme that they name: `pattern`: 0 or 1; every diagonal entry is 1. The first lengths[d] of the 12 slots of time device d are live.
All inputs are finite; a program needn't handle non-finite values.
Results may differ from the reference program's by a relative error of at most 0.0003.
Values sent between devices are 32-bit elements; how exact they have to be, the bound alone decides.
No kernel may reach another device: no remote copies, remote signals or barrier semaphores. Data moves between devices by JAX's collectives and lax.ppermute only.
A program may use at most 64 MiB of HBM per device.

```python
import math
import jax
import jax.numpy as jnp
import numpy as np
from jax import lax

STATE_SIZE = 512
NB = 8
TRACKS = 128
STEPS = 12
TIME_SLOTS = 192
N_TM = 16


def retention_rates(key):
    baseline_key, stride_key, spike_key, length_key = jax.random.split(key, 4)
    baseline_rate = jnp.exp(jax.random.uniform(baseline_key, (STATE_SIZE,), jnp.float32, jnp.log(0.0001), jnp.log(0.3)))
    multiplier = jax.random.uniform(stride_key, (TIME_SLOTS, STATE_SIZE), jnp.float32, 0.5, 1.5)
    spike_mask = jax.random.uniform(spike_key, (TIME_SLOTS, STATE_SIZE), jnp.float32) < 3.0 / TIME_SLOTS
    spike_length = jax.random.uniform(length_key, (TIME_SLOTS, STATE_SIZE), jnp.float32, 0.2, 0.5)
    return jnp.where(spike_mask, spike_length, baseline_rate[None, :] * multiplier)


def draw_gain(key, part):
    return retention_rates(jax.random.fold_in(key, 11))


def draw_smooth_gain(key, part):
    return 1.0 - retention_rates(jax.random.fold_in(key, 12))


def draw_dynamics(key, part):
    head_key, off_key = jax.random.split(jax.random.fold_in(key, 13))
    headroom = jnp.exp(jax.random.uniform(head_key, (STATE_SIZE,), jnp.float32, jnp.log(0.0002), jnp.log(0.04)))
    coupling = jnp.clip(0.5 * jax.random.normal(off_key, (STATE_SIZE, STATE_SIZE), jnp.float32), -1.0, 1.0)
    coupling_scale = 1.2 / STATE_SIZE ** 0.5
    eye_mask = jnp.eye(STATE_SIZE, dtype=jnp.float32)
    off_part = coupling_scale * headroom[:, None] * coupling
    return eye_mask * (1.0 - headroom)[None, :] + (1.0 - eye_mask) * off_part


def draw_pattern(key, part):
    coin_flips = jax.random.randint(jax.random.fold_in(key, 14), (NB, NB), 0, 2, dtype=jnp.int32)
    diagonal = jnp.arange(NB, dtype=jnp.int32)
    return jnp.where(diagonal[:, None] == diagonal[None, :], 1, coin_flips).astype(jnp.int32)


def levels(rng, dims, pieces, smallest, top_value):
    level = 1.0
    for axis_at, parts in pieces:
        steps = jax.random.uniform(jax.random.fold_in(jax.random.fold_in(rng, 6), axis_at), (parts,), jnp.float32, smallest / len(pieces), top_value / len(pieces))
        level = level * jnp.repeat(jnp.exp(steps), dims[axis_at] // parts).reshape((-1,) + (1,) * (len(dims) - 1 - axis_at))
    return level


def profile(amount, total, limit, skew):
    portions = [(1 << 20) // math.isqrt(standing ** skew) + 1 for standing in range(2, amount + 1)]
    surplus, holding = total - limit - (amount - 1), [1] * (amount - 1)
    while surplus > 0:
        free = [i for i in range(amount - 1) if holding[i] < limit]
        mass, left = sum([portions[i] for i in free]), surplus
        for i in free:
            extra = min(limit - holding[i], max(1, left * portions[i] // mass), surplus)
            holding[i] = holding[i] + extra
            surplus = surplus - extra
    return np.array([limit] + holding)


def uneven_parts(rng, number_of, total, limit, lean):
    if number_of == 2:
        one = jax.random.randint(rng, (), max(1, total - limit), min(limit, total - 1) + 1)
        return jnp.stack([one, total - one])
    sizes = jnp.asarray(profile(number_of, total, limit, lean), jnp.int32)
    twos = (number_of - 1) // 2
    donor, receiver = sizes[1:1 + 2 * twos:2], sizes[2:2 + 2 * twos:2]
    slack = jnp.minimum(donor - 1, limit - receiver)
    passed = jax.random.randint(jax.random.fold_in(rng, 1), (twos,), 0, 1 << 20) % (slack + 1)
    sizes = sizes.at[1:1 + 2 * twos:2].set(donor - passed).at[2:2 + 2 * twos:2].set(receiver + passed)
    return sizes[jax.random.permutation(jax.random.fold_in(rng, 2), number_of)]


def noise(key, extent, deviation, most, shards=(), kind=jnp.bfloat16):
    drawn = deviation * jax.random.normal(key, extent, jnp.float32)
    if shards:
        drawn = drawn * levels(key, extent, shards, -0.22, 0.18)
    return jnp.clip(drawn, -most, most).astype(kind)


def setup_inputs(seed: int = 0) -> dict:
    seeds = jax.random.split(jax.random.key(seed), 8)
    observed = noise(seeds[0], (TIME_SLOTS, STATE_SIZE, TRACKS), 2.0, 12.0, ((0, 16), (1, 2)), jnp.float32)
    gain = draw_gain(jax.random.fold_in(seeds[7], 71), 0)
    smooth_gain = draw_smooth_gain(jax.random.fold_in(seeds[7], 71), 0)
    dynamics = draw_dynamics(jax.random.fold_in(seeds[7], 71), 0)
    pattern = draw_pattern(jax.random.fold_in(seeds[7], 71), 0)
    initial = noise(seeds[5], (STATE_SIZE, TRACKS), 1.0, 6.0, ((0, 2),), jnp.float32)
    lengths = uneven_parts(seeds[6], N_TM, 3 * STEPS * N_TM // 4, STEPS, 2).astype(jnp.int32)
    return {"observed": observed, "gain": gain, "smooth_gain": smooth_gain, "dynamics": dynamics, "pattern": pattern, "initial": initial, "lengths": lengths}


HIGHEST = lax.Precision.HIGHEST


def product(left, right):
    return jnp.dot(left, right, precision=HIGHEST, preferred_element_type=jnp.float32)


def expand_pattern(pattern, dynamics):
    blocks = pattern.shape[0]
    block_width = dynamics.shape[0] // blocks
    spread = jnp.broadcast_to(pattern.astype(dynamics.dtype)[:, None, :, None], (blocks, block_width, blocks, block_width))
    return dynamics * spread.reshape(dynamics.shape)


def reference(observed, gain, smooth_gain, dynamics, pattern, initial, lengths):
    transition = expand_pattern(pattern, dynamics)
    slot_index = jnp.arange(STEPS * N_TM, dtype=jnp.int32)
    live_slots = (slot_index % STEPS) < lengths[slot_index // STEPS]

    def forward(previous, step_inputs):
        observation, gain_now, is_live = step_inputs
        image_now = product(transition, previous)
        updated = (1.0 - gain_now)[:, None] * image_now + gain_now[:, None] * observation
        current = jnp.where(is_live, updated, previous)
        return current, current

    final_mean, filtered = lax.scan(forward, initial, (observed, gain, live_slots))
    terminal = product(transition, final_mean)

    def backward(later_state, step_inputs):
        filtered_now, keep_now, is_live = step_inputs
        image_now = product(transition, filtered_now)
        offset = filtered_now - keep_now[:, None] * product(transition.T, image_now)
        updated = keep_now[:, None] * product(transition.T, later_state) + offset
        current = jnp.where(is_live, updated, later_state)
        return current, current

    first_state, smoothed = lax.scan(backward, terminal, (filtered, smooth_gain, live_slots), reverse=True)
    return filtered, smoothed
```

```python
import jax
import jax.numpy as jnp
from jax import lax
from jax.sharding import PartitionSpec as P

HIGHEST = lax.Precision.HIGHEST


def passed_along(block, axis, distance):
    devices = range(lax.axis_size(axis))
    route = [(i - distance, i) for i in devices if i - distance in devices]
    return lax.ppermute(block, axis, route)


def rows_whole(part, axis):
    count = lax.axis_size("rows")
    if count != 2:
        return lax.all_gather(part, "rows", axis=axis, tiled=True)
    other = lax.ppermute(part, "rows", [(0, 1), (1, 0)])
    first_half = lax.axis_index("rows") == 0
    lower = jnp.where(first_half, part, other)
    upper = jnp.where(first_half, other, part)
    return jnp.concatenate([lower, upper], axis=axis)


def matmul(left, right):
    return jnp.dot(left, right, precision=HIGHEST, preferred_element_type=jnp.float32)


def left_transposed(left, right):
    return lax.dot_general(
        left, right, (((0,), (0,)), ((), ())), precision=HIGHEST, preferred_element_type=jnp.float32
    )


def right_transposed(left, right):
    return lax.dot_general(
        left, right, (((1,), (1,)), ((), ())), precision=HIGHEST, preferred_element_type=jnp.float32
    )


def batched(left, right):
    return lax.dot_general(
        left, right, (((2,), (1,)), ((0,), (0,))), precision=HIGHEST, preferred_element_type=jnp.float32
    )


def masked_dynamics(pattern, dynamics):
    blocks = pattern.shape[0]
    block_width = dynamics.shape[0] // blocks
    spread = jnp.broadcast_to(
        pattern.astype(dynamics.dtype)[:, None, :, None], (blocks, block_width, blocks, block_width)
    )
    return dynamics * spread.reshape(dynamics.shape)


def lead_chain(start_rows, scales, live_slots, apply, backwards):
    def advance(lead, step_inputs):
        scale, is_live = step_inputs
        fresh = apply(lead * scale[None, :])
        return jnp.where(is_live, fresh, lead), lead

    return lax.scan(advance, start_rows, (scales, live_slots), reverse=backwards)


def lead_levels(lead, direction, devices, time_index):
    levels = (devices - 1).bit_length()
    leads = [lead]
    for tree_level in range(levels - 1):
        distance = 1 << tree_level
        far = rows_whole(passed_along(leads[-1], "tm", direction * distance), 0)
        has_peer = time_index >= distance if direction > 0 else time_index < devices - distance
        leads.append(jnp.where(has_peer, matmul(leads[-1], far), leads[-1]))
    return leads[:levels]


def offset_levels(offset, leads, direction, devices, time_index):
    for tree_level, lead in enumerate(leads):
        distance = 1 << tree_level
        far = rows_whole(passed_along(offset, "tm", direction * distance), 0)
        has_peer = time_index >= distance if direction > 0 else time_index < devices - distance
        offset = jnp.where(has_peer, offset + matmul(lead, far), offset)
    return offset


def per_device(observed, gain, smooth_gain, dynamics, pattern, initial, lengths):
    steps_local, row_count, tracks = observed.shape
    devices = lax.axis_size("tm")
    time_index = lax.axis_index("tm")
    row_start = lax.axis_index("rows") * row_count
    transition = masked_dynamics(pattern, dynamics)
    state_width = transition.shape[0]
    live_slots = jnp.arange(steps_local, dtype=jnp.int32) < lengths[0]
    column_ids = jnp.arange(state_width, dtype=jnp.int32)
    row_ids = row_start + jnp.arange(row_count, dtype=jnp.int32)
    identity_rows = (column_ids[None, :] == row_ids[:, None]).astype(jnp.float32)
    start_whole = lax.all_gather(initial, "rows", axis=0, tiled=True)
    obs_whole = lax.all_gather(observed, "rows", axis=1, tiled=True)
    at_first = time_index == 0
    at_last = time_index == devices - 1

    fwd_lead, fwd_before = lead_chain(
        identity_rows, 1.0 - gain, live_slots, lambda x: matmul(x, transition), True
    )
    fwd_leads = lead_levels(jnp.where(at_first, 0.0, fwd_lead), 1, devices, time_index)
    inputs = jnp.where(live_slots[:, None, None], gain[:, :, None] * obs_whole, 0.0)
    fwd_offset = jnp.sum(batched(fwd_before, inputs), axis=0)
    fwd_offset = jnp.where(at_first, fwd_offset + matmul(fwd_lead, start_whole), fwd_offset)
    fwd_inclusive = offset_levels(fwd_offset, fwd_leads, 1, devices, time_index)
    entry_rows = jnp.where(at_first, initial, passed_along(fwd_inclusive, "tm", 1))
    entry_whole = rows_whole(entry_rows, 0)

    back_lead, back_before = lead_chain(
        identity_rows, smooth_gain, live_slots, lambda x: right_transposed(x, transition), False
    )
    back_leads = lead_levels(jnp.where(at_last, 0.0, back_lead), -1, devices, time_index)

    def forward(mean_whole, step_inputs):
        obs_now, rate_now, is_live = step_inputs
        image_now = matmul(transition, mean_whole)
        fresh = (1.0 - rate_now)[:, None] * image_now + rate_now[:, None] * obs_now
        mean_next = jnp.where(is_live, fresh, mean_whole)
        return mean_next, (mean_next, image_now)

    final_mean, (filtered_whole, images) = lax.scan(
        forward, entry_whole, (obs_whole, gain, live_slots)
    )
    terminal = matmul(transition, final_mean)
    image_all = jnp.concatenate([images[1:], terminal[None]], axis=0)
    pulled = jnp.einsum("ji,tjk->tik", transition, image_all, precision=HIGHEST,
                        preferred_element_type=jnp.float32)
    offsets = filtered_whole - smooth_gain[:, :, None] * pulled

    live_offsets = jnp.where(live_slots[:, None, None], offsets, 0.0)
    back_offset = jnp.sum(batched(back_before, live_offsets), axis=0)
    back_offset = jnp.where(at_last, back_offset + matmul(back_lead, terminal), back_offset)
    back_inclusive = offset_levels(back_offset, back_leads, -1, devices, time_index)
    terminal_rows = lax.dynamic_slice_in_dim(terminal, row_start, row_count, 0)
    after_rows = jnp.where(at_last, terminal_rows, passed_along(back_inclusive, "tm", -1))
    after_whole = rows_whole(after_rows, 0)

    def backward(later_whole, step_inputs):
        offset_now, keep_now, is_live = step_inputs
        fresh = keep_now[:, None] * left_transposed(transition, later_whole) + offset_now
        smooth_now = jnp.where(is_live, fresh, later_whole)
        return smooth_now, smooth_now

    first_whole, smoothed_whole = lax.scan(
        backward, after_whole, (offsets, smooth_gain, live_slots), reverse=True
    )
    filtered = lax.dynamic_slice_in_dim(filtered_whole, row_start, row_count, 1)
    smoothed = lax.dynamic_slice_in_dim(smoothed_whole, row_start, row_count, 1)
    return (filtered, smoothed)


def solution(mesh):
    placed = (
        P("tm", "rows", None),
        P("tm", None),
        P("tm", None),
        P(),
        P(),
        P("rows", None),
        P("tm"),
    )
    return jax.shard_map(
        per_device,
        mesh=mesh,
        in_specs=placed,
        out_specs=(P("tm", "rows", None), P("tm", "rows", None)),
        check_vma=False,
    )
```

```python
import jax
import jax.numpy as jnp
from jax import lax
from jax.sharding import PartitionSpec as P

HIGHEST = lax.Precision.HIGHEST


def passed_along(block, axis, distance):
    devices = range(lax.axis_size(axis))
    route = [(i - distance, i) for i in devices if i - distance in devices]
    return lax.ppermute(block, axis, route)


def rows_whole(part, axis):
    count = lax.axis_size("rows")
    if count != 2:
        return lax.all_gather(part, "rows", axis=axis, tiled=True)
    other = lax.ppermute(part, "rows", [(0, 1), (1, 0)])
    first_half = lax.axis_index("rows") == 0
    lower = jnp.where(first_half, part, other)
    upper = jnp.where(first_half, other, part)
    return jnp.concatenate([lower, upper], axis=axis)


def matmul(left, right):
    return jnp.dot(left, right, precision=HIGHEST, preferred_element_type=jnp.float32)


def left_transposed(left, right):
    return lax.dot_general(
        left, right, (((0,), (0,)), ((), ())), precision=HIGHEST, preferred_element_type=jnp.float32
    )


def right_transposed(left, right):
    return lax.dot_general(
        left, right, (((1,), (1,)), ((), ())), precision=HIGHEST, preferred_element_type=jnp.float32
    )


def batched(left, right):
    return lax.dot_general(
        left, right, (((2,), (1,)), ((0,), (0,))), precision=HIGHEST, preferred_element_type=jnp.float32
    )


def masked_dynamics(pattern, dynamics):
    blocks = pattern.shape[0]
    block_width = dynamics.shape[0] // blocks
    spread = jnp.broadcast_to(
        pattern.astype(dynamics.dtype)[:, None, :, None], (blocks, block_width, blocks, block_width)
    )
    return dynamics * spread.reshape(dynamics.shape)


def lead_chain(start_rows, scales, live_slots, apply, backwards):
    def advance(lead, step_inputs):
        scale, is_live = step_inputs
        fresh = apply(lead * scale[None, :])
        return jnp.where(is_live, fresh, lead), lead

    return lax.scan(advance, start_rows, (scales, live_slots), reverse=backwards, unroll=True)


def lead_levels(lead, direction, devices, time_index):
    levels = (devices - 1).bit_length()
    leads = [lead]
    for tree_level in range(levels - 1):
        distance = 1 << tree_level
        far = rows_whole(passed_along(leads[-1], "tm", direction * distance), 0)
        has_peer = time_index >= distance if direction > 0 else time_index < devices - distance
        leads.append(jnp.where(has_peer, matmul(leads[-1], far), leads[-1]))
    return leads[:levels]


def offset_levels(offset, leads, direction, devices, time_index):
    for tree_level, lead in enumerate(leads):
        distance = 1 << tree_level
        far = rows_whole(passed_along(offset, "tm", direction * distance), 0)
        has_peer = time_index >= distance if direction > 0 else time_index < devices - distance
        offset = jnp.where(has_peer, offset + matmul(lead, far), offset)
    return offset


def per_device(observed, gain, smooth_gain, dynamics, pattern, initial, lengths):
    steps_local, row_count, tracks = observed.shape
    devices = lax.axis_size("tm")
    time_index = lax.axis_index("tm")
    row_start = lax.axis_index("rows") * row_count
    transition = masked_dynamics(pattern, dynamics)
    state_width = transition.shape[0]
    live_slots = jnp.arange(steps_local, dtype=jnp.int32) < lengths[0]
    column_ids = jnp.arange(state_width, dtype=jnp.int32)
    row_ids = row_start + jnp.arange(row_count, dtype=jnp.int32)
    identity_rows = (column_ids[None, :] == row_ids[:, None]).astype(jnp.float32)
    start_whole = lax.all_gather(initial, "rows", axis=0, tiled=True)
    obs_whole = lax.all_gather(observed, "rows", axis=1, tiled=True)
    at_first = time_index == 0
    at_last = time_index == devices - 1

    fwd_lead, fwd_before = lead_chain(
        identity_rows, 1.0 - gain, live_slots, lambda x: matmul(x, transition), True
    )
    fwd_leads = lead_levels(jnp.where(at_first, 0.0, fwd_lead), 1, devices, time_index)
    inputs = jnp.where(live_slots[:, None, None], gain[:, :, None] * obs_whole, 0.0)
    fwd_offset = jnp.sum(batched(fwd_before, inputs), axis=0)
    fwd_offset = jnp.where(at_first, fwd_offset + matmul(fwd_lead, start_whole), fwd_offset)
    fwd_inclusive = offset_levels(fwd_offset, fwd_leads, 1, devices, time_index)
    entry_rows = jnp.where(at_first, initial, passed_along(fwd_inclusive, "tm", 1))
    entry_whole = rows_whole(entry_rows, 0)

    back_lead, back_before = lead_chain(
        identity_rows, smooth_gain, live_slots, lambda x: right_transposed(x, transition), False
    )
    back_leads = lead_levels(jnp.where(at_last, 0.0, back_lead), -1, devices, time_index)

    def forward(mean_whole, step_inputs):
        obs_now, rate_now, is_live = step_inputs
        image_now = matmul(transition, mean_whole)
        fresh = (1.0 - rate_now)[:, None] * image_now + rate_now[:, None] * obs_now
        mean_next = jnp.where(is_live, fresh, mean_whole)
        return mean_next, (mean_next, image_now)

    final_mean, (filtered_whole, images) = lax.scan(
        forward, entry_whole, (obs_whole, gain, live_slots), unroll=True
    )
    terminal = matmul(transition, final_mean)
    image_all = jnp.concatenate([images[1:], terminal[None]], axis=0)
    pulled = jnp.einsum("ji,tjk->tik", transition, image_all, precision=HIGHEST,
                        preferred_element_type=jnp.float32)
    offsets = filtered_whole - smooth_gain[:, :, None] * pulled

    live_offsets = jnp.where(live_slots[:, None, None], offsets, 0.0)
    back_offset = jnp.sum(batched(back_before, live_offsets), axis=0)
    back_offset = jnp.where(at_last, back_offset + matmul(back_lead, terminal), back_offset)
    back_inclusive = offset_levels(back_offset, back_leads, -1, devices, time_index)
    terminal_rows = lax.dynamic_slice_in_dim(terminal, row_start, row_count, 0)
    after_rows = jnp.where(at_last, terminal_rows, passed_along(back_inclusive, "tm", -1))
    after_whole = rows_whole(after_rows, 0)

    def backward(later_whole, step_inputs):
        offset_now, keep_now, is_live = step_inputs
        fresh = keep_now[:, None] * left_transposed(transition, later_whole) + offset_now
        smooth_now = jnp.where(is_live, fresh, later_whole)
        return smooth_now, smooth_now

    first_whole, smoothed_whole = lax.scan(
        backward, after_whole, (offsets, smooth_gain, live_slots), reverse=True, unroll=True
    )
    filtered = lax.dynamic_slice_in_dim(filtered_whole, row_start, row_count, 1)
    smoothed = lax.dynamic_slice_in_dim(smoothed_whole, row_start, row_count, 1)
    return (filtered, smoothed)


def solution(mesh):
    placed = (
        P("tm", "rows", None),
        P("tm", None),
        P("tm", None),
        P(),
        P(),
        P("rows", None),
        P("tm"),
    )
    return jax.shard_map(
        per_device,
        mesh=mesh,
        in_specs=placed,
        out_specs=(P("tm", "rows", None), P("tm", "rows", None)),
        check_vma=False,
    )
```

```python
import jax
import jax.numpy as jnp
from jax import lax
from jax.sharding import PartitionSpec as P

HIGHEST = lax.Precision.HIGHEST


def passed_along(block, axis, distance):
    devices = range(lax.axis_size(axis))
    route = [(i - distance, i) for i in devices if i - distance in devices]
    return lax.ppermute(block, axis, route)


def rows_whole(part, axis):
    count = lax.axis_size("rows")
    if count != 2:
        return lax.all_gather(part, "rows", axis=axis, tiled=True)
    other = lax.ppermute(part, "rows", [(0, 1), (1, 0)])
    first_half = lax.axis_index("rows") == 0
    lower = jnp.where(first_half, part, other)
    upper = jnp.where(first_half, other, part)
    return jnp.concatenate([lower, upper], axis=axis)


def far_whole(block, distance):
    if lax.axis_size("rows") != 2:
        return rows_whole(passed_along(block, "tm", distance), 0)
    count = lax.axis_size("tm")
    axes = ("tm", "rows")
    same, cross = [], []
    for i in range(count):
        if 0 <= i - distance < count:
            for r in range(2):
                same.append(((i - distance) * 2 + r, i * 2 + r))
                cross.append(((i - distance) * 2 + 1 - r, i * 2 + r))
    mine = lax.ppermute(block, axes, same)
    other = lax.ppermute(block, axes, cross)
    first_half = lax.axis_index("rows") == 0
    lower = jnp.where(first_half, mine, other)
    upper = jnp.where(first_half, other, mine)
    return jnp.concatenate([lower, upper], axis=0)


def matmul(left, right):
    return jnp.dot(left, right, precision=HIGHEST, preferred_element_type=jnp.float32)


def left_transposed(left, right):
    return lax.dot_general(
        left, right, (((0,), (0,)), ((), ())), precision=HIGHEST, preferred_element_type=jnp.float32
    )


def right_transposed(left, right):
    return lax.dot_general(
        left, right, (((1,), (1,)), ((), ())), precision=HIGHEST, preferred_element_type=jnp.float32
    )


def batched(left, right):
    return lax.dot_general(
        left, right, (((2,), (1,)), ((0,), (0,))), precision=HIGHEST, preferred_element_type=jnp.float32
    )


def masked_dynamics(pattern, dynamics):
    blocks = pattern.shape[0]
    block_width = dynamics.shape[0] // blocks
    spread = jnp.broadcast_to(
        pattern.astype(dynamics.dtype)[:, None, :, None], (blocks, block_width, blocks, block_width)
    )
    return dynamics * spread.reshape(dynamics.shape)


def lead_chain(start_rows, scales, live_slots, apply, backwards):
    def advance(lead, step_inputs):
        scale, is_live = step_inputs
        fresh = apply(lead * scale[None, :])
        return jnp.where(is_live, fresh, lead), lead

    return lax.scan(advance, start_rows, (scales, live_slots), reverse=backwards, unroll=True)


def lead_levels(lead, direction, devices, time_index):
    levels = (devices - 1).bit_length()
    leads = [lead]
    for tree_level in range(levels - 1):
        distance = 1 << tree_level
        far = rows_whole(passed_along(leads[-1], "tm", direction * distance), 0)
        has_peer = time_index >= distance if direction > 0 else time_index < devices - distance
        leads.append(jnp.where(has_peer, matmul(leads[-1], far), leads[-1]))
    return leads[:levels]


def offset_levels(offset, leads, direction, devices, time_index):
    for tree_level, lead in enumerate(leads):
        distance = 1 << tree_level
        far = far_whole(offset, direction * distance)
        has_peer = time_index >= distance if direction > 0 else time_index < devices - distance
        offset = jnp.where(has_peer, offset + matmul(lead, far), offset)
    return offset


def per_device(observed, gain, smooth_gain, dynamics, pattern, initial, lengths):
    steps_local, row_count, tracks = observed.shape
    devices = lax.axis_size("tm")
    time_index = lax.axis_index("tm")
    row_start = lax.axis_index("rows") * row_count
    transition = masked_dynamics(pattern, dynamics)
    transposed = transition.T
    state_width = transition.shape[0]
    live_slots = jnp.arange(steps_local, dtype=jnp.int32) < lengths[0]
    column_ids = jnp.arange(state_width, dtype=jnp.int32)
    row_ids = row_start + jnp.arange(row_count, dtype=jnp.int32)
    identity_rows = (column_ids[None, :] == row_ids[:, None]).astype(jnp.float32)
    start_whole = lax.all_gather(initial, "rows", axis=0, tiled=True)
    obs_whole = lax.all_gather(observed, "rows", axis=1, tiled=True)
    at_first = time_index == 0
    at_last = time_index == devices - 1

    fwd_lead, fwd_before = lead_chain(
        identity_rows, 1.0 - gain, live_slots, lambda x: matmul(x, transition), True
    )
    fwd_leads = lead_levels(jnp.where(at_first, 0.0, fwd_lead), 1, devices, time_index)
    inputs = jnp.where(live_slots[:, None, None], gain[:, :, None] * obs_whole, 0.0)
    fwd_offset = jnp.sum(batched(fwd_before, inputs), axis=0)
    fwd_offset = jnp.where(at_first, fwd_offset + matmul(fwd_lead, start_whole), fwd_offset)
    fwd_inclusive = offset_levels(fwd_offset, fwd_leads, 1, devices, time_index)
    entry_whole = jnp.where(at_first, start_whole, far_whole(fwd_inclusive, 1))

    back_lead, back_before = lead_chain(
        identity_rows, smooth_gain, live_slots, lambda x: matmul(x, transposed), False
    )
    back_leads = lead_levels(jnp.where(at_last, 0.0, back_lead), -1, devices, time_index)

    def forward(mean_whole, step_inputs):
        obs_now, rate_now, is_live = step_inputs
        image_now = matmul(transition, mean_whole)
        fresh = (1.0 - rate_now)[:, None] * image_now + rate_now[:, None] * obs_now
        mean_next = jnp.where(is_live, fresh, mean_whole)
        return mean_next, (mean_next, image_now)

    final_mean, (filtered_whole, images) = lax.scan(
        forward, entry_whole, (obs_whole, gain, live_slots), unroll=True
    )
    terminal = matmul(transition, final_mean)
    image_all = jnp.concatenate([images[1:], terminal[None]], axis=0)
    pulled = jnp.einsum("ij,tjk->tik", transposed, image_all, precision=HIGHEST,
                        preferred_element_type=jnp.float32)
    offsets = filtered_whole - smooth_gain[:, :, None] * pulled

    live_offsets = jnp.where(live_slots[:, None, None], offsets, 0.0)
    back_offset = jnp.sum(batched(back_before, live_offsets), axis=0)
    back_offset = jnp.where(at_last, back_offset + matmul(back_lead, terminal), back_offset)
    back_inclusive = offset_levels(back_offset, back_leads, -1, devices, time_index)
    after_whole = jnp.where(at_last, terminal, far_whole(back_inclusive, -1))

    def backward(later_whole, step_inputs):
        offset_now, keep_now, is_live = step_inputs
        fresh = keep_now[:, None] * matmul(transposed, later_whole) + offset_now
        smooth_now = jnp.where(is_live, fresh, later_whole)
        return smooth_now, smooth_now

    first_whole, smoothed_whole = lax.scan(
        backward, after_whole, (offsets, smooth_gain, live_slots), reverse=True, unroll=True
    )
    filtered = lax.dynamic_slice_in_dim(filtered_whole, row_start, row_count, 1)
    smoothed = lax.dynamic_slice_in_dim(smoothed_whole, row_start, row_count, 1)
    return (filtered, smoothed)


def solution(mesh):
    placed = (
        P("tm", "rows", None),
        P("tm", None),
        P("tm", None),
        P(),
        P(),
        P("rows", None),
        P("tm"),
    )
    return jax.shard_map(
        per_device,
        mesh=mesh,
        in_specs=placed,
        out_specs=(P("tm", "rows", None), P("tm", "rows", None)),
        check_vma=False,
    )
```

```python
import jax
import jax.numpy as jnp
from jax import lax
from jax.sharding import PartitionSpec as P

HIGHEST = lax.Precision.HIGHEST


def passed_along(block, axis, distance):
    devices = range(lax.axis_size(axis))
    route = [(i - distance, i) for i in devices if i - distance in devices]
    return lax.ppermute(block, axis, route)


def rows_whole(part, axis):
    count = lax.axis_size("rows")
    if count != 2:
        return lax.all_gather(part, "rows", axis=axis, tiled=True)
    other = lax.ppermute(part, "rows", [(0, 1), (1, 0)])
    first_half = lax.axis_index("rows") == 0
    lower = jnp.where(first_half, part, other)
    upper = jnp.where(first_half, other, part)
    return jnp.concatenate([lower, upper], axis=axis)


def matmul(left, right):
    return jnp.dot(left, right, precision=HIGHEST, preferred_element_type=jnp.float32)


def left_transposed(left, right):
    return lax.dot_general(
        left, right, (((0,), (0,)), ((), ())), precision=HIGHEST, preferred_element_type=jnp.float32
    )


def right_transposed(left, right):
    return lax.dot_general(
        left, right, (((1,), (1,)), ((), ())), precision=HIGHEST, preferred_element_type=jnp.float32
    )


def batched(left, right):
    return lax.dot_general(
        left, right, (((2,), (1,)), ((0,), (0,))), precision=HIGHEST, preferred_element_type=jnp.float32
    )


def masked_dynamics(pattern, dynamics):
    blocks = pattern.shape[0]
    block_width = dynamics.shape[0] // blocks
    spread = jnp.broadcast_to(
        pattern.astype(dynamics.dtype)[:, None, :, None], (blocks, block_width, blocks, block_width)
    )
    return dynamics * spread.reshape(dynamics.shape)


def lead_chain(start_rows, scales, live_slots, apply, backwards):
    def advance(lead, step_inputs):
        scale, is_live = step_inputs
        fresh = apply(lead * scale[None, :])
        return jnp.where(is_live, fresh, lead), lead

    return lax.scan(advance, start_rows, (scales, live_slots), reverse=backwards, unroll=True)


def prefix_tree(lead, offset, direction, devices, time_index):
    levels = (devices - 1).bit_length()
    width = lead.shape[1]
    for tree_level in range(levels):
        distance = 1 << tree_level
        has_peer = time_index >= distance if direction > 0 else time_index < devices - distance
        if tree_level < levels - 1:
            both = jnp.concatenate([lead, offset], axis=1)
            far = rows_whole(passed_along(both, "tm", direction * distance), 0)
            joined = matmul(lead, far)
            lead = jnp.where(has_peer, joined[:, :width], lead)
            offset = jnp.where(has_peer, offset + joined[:, width:], offset)
        else:
            far = rows_whole(passed_along(offset, "tm", direction * distance), 0)
            offset = jnp.where(has_peer, offset + matmul(lead, far), offset)
    return offset


def per_device(observed, gain, smooth_gain, dynamics, pattern, initial, lengths):
    steps_local, row_count, tracks = observed.shape
    devices = lax.axis_size("tm")
    time_index = lax.axis_index("tm")
    row_start = lax.axis_index("rows") * row_count
    transition = masked_dynamics(pattern, dynamics)
    transposed = transition.T
    state_width = transition.shape[0]
    live_slots = jnp.arange(steps_local, dtype=jnp.int32) < lengths[0]
    column_ids = jnp.arange(state_width, dtype=jnp.int32)
    row_ids = row_start + jnp.arange(row_count, dtype=jnp.int32)
    identity_rows = (column_ids[None, :] == row_ids[:, None]).astype(jnp.float32)
    start_whole = lax.all_gather(initial, "rows", axis=0, tiled=True)
    obs_whole = lax.all_gather(observed, "rows", axis=1, tiled=True)
    at_first = time_index == 0
    at_last = time_index == devices - 1

    fwd_lead, fwd_before = lead_chain(
        identity_rows, 1.0 - gain, live_slots, lambda x: matmul(x, transition), True
    )
    inputs = jnp.where(live_slots[:, None, None], gain[:, :, None] * obs_whole, 0.0)
    fwd_offset = jnp.sum(batched(fwd_before, inputs), axis=0)
    fwd_offset = jnp.where(at_first, fwd_offset + matmul(fwd_lead, start_whole), fwd_offset)
    fwd_inclusive = prefix_tree(
        jnp.where(at_first, 0.0, fwd_lead), fwd_offset, 1, devices, time_index
    )
    entry_rows = jnp.where(at_first, initial, passed_along(fwd_inclusive, "tm", 1))
    entry_whole = rows_whole(entry_rows, 0)

    back_lead, back_before = lead_chain(
        identity_rows, smooth_gain, live_slots, lambda x: matmul(x, transposed), False
    )

    def forward(mean_whole, step_inputs):
        obs_now, rate_now, is_live = step_inputs
        image_now = matmul(transition, mean_whole)
        fresh = (1.0 - rate_now)[:, None] * image_now + rate_now[:, None] * obs_now
        mean_next = jnp.where(is_live, fresh, mean_whole)
        return mean_next, (mean_next, image_now)

    final_mean, (filtered_whole, images) = lax.scan(
        forward, entry_whole, (obs_whole, gain, live_slots), unroll=True
    )
    terminal = matmul(transition, final_mean)
    image_all = jnp.concatenate([images[1:], terminal[None]], axis=0)
    pulled = jnp.einsum("ij,tjk->tik", transposed, image_all, precision=HIGHEST,
                        preferred_element_type=jnp.float32)
    offsets = filtered_whole - smooth_gain[:, :, None] * pulled

    live_offsets = jnp.where(live_slots[:, None, None], offsets, 0.0)
    back_offset = jnp.sum(batched(back_before, live_offsets), axis=0)
    back_offset = jnp.where(at_last, back_offset + matmul(back_lead, terminal), back_offset)
    back_inclusive = prefix_tree(
        jnp.where(at_last, 0.0, back_lead), back_offset, -1, devices, time_index
    )
    terminal_rows = lax.dynamic_slice_in_dim(terminal, row_start, row_count, 0)
    after_rows = jnp.where(at_last, terminal_rows, passed_along(back_inclusive, "tm", -1))
    after_whole = rows_whole(after_rows, 0)

    def backward(later_whole, step_inputs):
        offset_now, keep_now, is_live = step_inputs
        fresh = keep_now[:, None] * matmul(transposed, later_whole) + offset_now
        smooth_now = jnp.where(is_live, fresh, later_whole)
        return smooth_now, smooth_now

    first_whole, smoothed_whole = lax.scan(
        backward, after_whole, (offsets, smooth_gain, live_slots), reverse=True, unroll=True
    )
    filtered = lax.dynamic_slice_in_dim(filtered_whole, row_start, row_count, 1)
    smoothed = lax.dynamic_slice_in_dim(smoothed_whole, row_start, row_count, 1)
    return (filtered, smoothed)


def solution(mesh):
    placed = (
        P("tm", "rows", None),
        P("tm", None),
        P("tm", None),
        P(),
        P(),
        P("rows", None),
        P("tm"),
    )
    return jax.shard_map(
        per_device,
        mesh=mesh,
        in_specs=placed,
        out_specs=(P("tm", "rows", None), P("tm", "rows", None)),
        check_vma=False,
    )
```

```python
import jax
import jax.numpy as jnp
from jax import lax
from jax.sharding import PartitionSpec as P

HIGHEST = lax.Precision.HIGHEST


def passed_along(block, axis, distance):
    devices = range(lax.axis_size(axis))
    route = [(i - distance, i) for i in devices if i - distance in devices]
    return lax.ppermute(block, axis, route)


def rows_whole(part, axis):
    count = lax.axis_size("rows")
    if count != 2:
        return lax.all_gather(part, "rows", axis=axis, tiled=True)
    other = lax.ppermute(part, "rows", [(0, 1), (1, 0)])
    first_half = lax.axis_index("rows") == 0
    lower = jnp.where(first_half, part, other)
    upper = jnp.where(first_half, other, part)
    return jnp.concatenate([lower, upper], axis=axis)


def matmul(left, right):
    return jnp.dot(left, right, precision=HIGHEST, preferred_element_type=jnp.float32)


def left_transposed(left, right):
    return lax.dot_general(
        left, right, (((0,), (0,)), ((), ())), precision=HIGHEST, preferred_element_type=jnp.float32
    )


def right_transposed(left, right):
    return lax.dot_general(
        left, right, (((1,), (1,)), ((), ())), precision=HIGHEST, preferred_element_type=jnp.float32
    )


def batched(left, right):
    return lax.dot_general(
        left, right, (((2,), (1,)), ((0,), (0,))), precision=HIGHEST, preferred_element_type=jnp.float32
    )


def masked_dynamics(pattern, dynamics):
    blocks = pattern.shape[0]
    block_width = dynamics.shape[0] // blocks
    spread = jnp.broadcast_to(
        pattern.astype(dynamics.dtype)[:, None, :, None], (blocks, block_width, blocks, block_width)
    )
    return dynamics * spread.reshape(dynamics.shape)


def lead_chain(start_rows, scales, live_slots, apply, backwards):
    def advance(lead, step_inputs):
        scale, is_live = step_inputs
        fresh = apply(lead * scale[None, :])
        return jnp.where(is_live, fresh, lead), lead

    return lax.scan(advance, start_rows, (scales, live_slots), reverse=backwards, unroll=True)


def lead_levels(lead, direction, devices, time_index):
    levels = (devices - 1).bit_length()
    leads = [lead]
    for tree_level in range(levels - 1):
        distance = 1 << tree_level
        far = rows_whole(passed_along(leads[-1], "tm", direction * distance), 0)
        has_peer = time_index >= distance if direction > 0 else time_index < devices - distance
        leads.append(jnp.where(has_peer, matmul(leads[-1], far), leads[-1]))
    return leads[:levels]


def offset_levels(offset, leads, direction, devices, time_index):
    for tree_level, lead in enumerate(leads):
        distance = 1 << tree_level
        far = rows_whole(passed_along(offset, "tm", direction * distance), 0)
        has_peer = time_index >= distance if direction > 0 else time_index < devices - distance
        offset = jnp.where(has_peer, offset + matmul(lead, far), offset)
    return offset


def exit_levels(offset, leads, next_lead, direction, devices, time_index):
    for tree_level, lead in enumerate(leads[:-1]):
        distance = 1 << tree_level
        far = rows_whole(passed_along(offset, "tm", direction * distance), 0)
        has_peer = time_index >= distance if direction > 0 else time_index < devices - distance
        offset = jnp.where(has_peer, offset + matmul(lead, far), offset)
    distance = 1 << (len(leads) - 1)
    near = passed_along(offset, "tm", direction)
    far = rows_whole(passed_along(offset, "tm", direction * (distance + 1)), 0)
    neighbour = time_index - direction
    has_peer = neighbour >= distance if direction > 0 else neighbour < devices - distance
    return jnp.where(has_peer, near + matmul(next_lead, far), near)


def per_device(observed, gain, smooth_gain, dynamics, pattern, initial, lengths):
    steps_local, row_count, tracks = observed.shape
    devices = lax.axis_size("tm")
    time_index = lax.axis_index("tm")
    row_start = lax.axis_index("rows") * row_count
    transition = masked_dynamics(pattern, dynamics)
    transposed = transition.T
    state_width = transition.shape[0]
    live_slots = jnp.arange(steps_local, dtype=jnp.int32) < lengths[0]
    column_ids = jnp.arange(state_width, dtype=jnp.int32)
    row_ids = row_start + jnp.arange(row_count, dtype=jnp.int32)
    identity_rows = (column_ids[None, :] == row_ids[:, None]).astype(jnp.float32)
    start_whole = lax.all_gather(initial, "rows", axis=0, tiled=True)
    obs_whole = lax.all_gather(observed, "rows", axis=1, tiled=True)
    at_first = time_index == 0
    at_last = time_index == devices - 1

    prev_observed = passed_along(observed, "tm", 1)
    prev_gain = passed_along(gain, "tm", 1)
    prev_live = jnp.arange(steps_local, dtype=jnp.int32) < passed_along(lengths, "tm", 1)[0]
    prev_obs_whole = lax.all_gather(prev_observed, "rows", axis=1, tiled=True)
    prev_lead, prev_before = lead_chain(
        identity_rows, 1.0 - prev_gain, prev_live, lambda x: matmul(x, transition), True
    )
    prev_inputs = jnp.where(prev_live[:, None, None], prev_gain[:, :, None] * prev_obs_whole, 0.0)
    prev_offset = jnp.sum(batched(prev_before, prev_inputs), axis=0)
    fwd_leads = lead_levels(jnp.where(at_first, 0.0, prev_lead), 1, devices, time_index)
    entry_rows = offset_levels(
        jnp.where(at_first, initial, prev_offset), fwd_leads, 1, devices, time_index
    )
    entry_whole = rows_whole(entry_rows, 0)

    back_lead, back_before = lead_chain(
        identity_rows, smooth_gain, live_slots, lambda x: matmul(x, transposed), False
    )
    back_leads = lead_levels(jnp.where(at_last, 0.0, back_lead), -1, devices, time_index)
    next_lead = passed_along(back_leads[-1], "tm", -1)

    def forward(mean_whole, step_inputs):
        obs_now, rate_now, is_live = step_inputs
        image_now = matmul(transition, mean_whole)
        fresh = (1.0 - rate_now)[:, None] * image_now + rate_now[:, None] * obs_now
        mean_next = jnp.where(is_live, fresh, mean_whole)
        return mean_next, (mean_next, image_now)

    final_mean, (filtered_whole, images) = lax.scan(
        forward, entry_whole, (obs_whole, gain, live_slots), unroll=True
    )
    terminal = matmul(transition, final_mean)
    image_all = jnp.concatenate([images[1:], terminal[None]], axis=0)
    pulled = jnp.einsum("ij,tjk->tik", transposed, image_all, precision=HIGHEST,
                        preferred_element_type=jnp.float32)
    offsets = filtered_whole - smooth_gain[:, :, None] * pulled

    live_offsets = jnp.where(live_slots[:, None, None], offsets, 0.0)
    back_offset = jnp.sum(batched(back_before, live_offsets), axis=0)
    back_offset = jnp.where(at_last, back_offset + matmul(back_lead, terminal), back_offset)
    next_inclusive = exit_levels(back_offset, back_leads, next_lead, -1, devices, time_index)
    terminal_rows = lax.dynamic_slice_in_dim(terminal, row_start, row_count, 0)
    after_rows = jnp.where(at_last, terminal_rows, next_inclusive)
    after_whole = rows_whole(after_rows, 0)

    def backward(later_whole, step_inputs):
        offset_now, keep_now, is_live = step_inputs
        fresh = keep_now[:, None] * matmul(transposed, later_whole) + offset_now
        smooth_now = jnp.where(is_live, fresh, later_whole)
        return smooth_now, smooth_now

    first_whole, smoothed_whole = lax.scan(
        backward, after_whole, (offsets, smooth_gain, live_slots), reverse=True, unroll=True
    )
    filtered = lax.dynamic_slice_in_dim(filtered_whole, row_start, row_count, 1)
    smoothed = lax.dynamic_slice_in_dim(smoothed_whole, row_start, row_count, 1)
    return (filtered, smoothed)


def solution(mesh):
    placed = (
        P("tm", "rows", None),
        P("tm", None),
        P("tm", None),
        P(),
        P(),
        P("rows", None),
        P("tm"),
    )
    return jax.shard_map(
        per_device,
        mesh=mesh,
        in_specs=placed,
        out_specs=(P("tm", "rows", None), P("tm", "rows", None)),
        check_vma=False,
    )
```

```python
import jax
import jax.numpy as jnp
from jax import lax
from jax.sharding import PartitionSpec as P

HIGHEST = lax.Precision.HIGHEST


def passed_along(block, axis, distance):
    devices = range(lax.axis_size(axis))
    route = [(i - distance, i) for i in devices if i - distance in devices]
    return lax.ppermute(block, axis, route)


def passed_across(block, distance):
    count, cores = lax.axis_size("tm"), lax.axis_size("rows")
    route = [
        ((i - distance) * cores + (cores - 1 - r), i * cores + r)
        for i in range(count)
        if 0 <= i - distance < count
        for r in range(cores)
    ]
    return lax.ppermute(block, ("tm", "rows"), route)


def rows_whole(part, axis):
    count = lax.axis_size("rows")
    if count != 2:
        return lax.all_gather(part, "rows", axis=axis, tiled=True)
    other = lax.ppermute(part, "rows", [(0, 1), (1, 0)])
    first_half = lax.axis_index("rows") == 0
    lower = jnp.where(first_half, part, other)
    upper = jnp.where(first_half, other, part)
    return jnp.concatenate([lower, upper], axis=axis)


def matmul(left, right):
    return jnp.dot(left, right, precision=HIGHEST, preferred_element_type=jnp.float32)


def left_transposed(left, right):
    return lax.dot_general(
        left, right, (((0,), (0,)), ((), ())), precision=HIGHEST, preferred_element_type=jnp.float32
    )


def right_transposed(left, right):
    return lax.dot_general(
        left, right, (((1,), (1,)), ((), ())), precision=HIGHEST, preferred_element_type=jnp.float32
    )


def batched(left, right):
    return lax.dot_general(
        left, right, (((2,), (1,)), ((0,), (0,))), precision=HIGHEST, preferred_element_type=jnp.float32
    )


def masked_dynamics(pattern, dynamics):
    blocks = pattern.shape[0]
    block_width = dynamics.shape[0] // blocks
    spread = jnp.broadcast_to(
        pattern.astype(dynamics.dtype)[:, None, :, None], (blocks, block_width, blocks, block_width)
    )
    return dynamics * spread.reshape(dynamics.shape)


def lead_chain(start_rows, scales, live_slots, apply, backwards):
    def advance(lead, step_inputs):
        scale, is_live = step_inputs
        fresh = apply(lead * scale[None, :])
        return jnp.where(is_live, fresh, lead), lead

    return lax.scan(advance, start_rows, (scales, live_slots), reverse=backwards, unroll=True)


def lead_levels(lead, direction, devices, time_index):
    levels = (devices - 1).bit_length()
    leads = [lead]
    for tree_level in range(levels - 1):
        distance = 1 << tree_level
        far = rows_whole(passed_along(leads[-1], "tm", direction * distance), 0)
        has_peer = time_index >= distance if direction > 0 else time_index < devices - distance
        leads.append(jnp.where(has_peer, matmul(leads[-1], far), leads[-1]))
    return leads[:levels]


def offset_levels(offset, leads, direction, devices, time_index):
    for tree_level, lead in enumerate(leads):
        distance = 1 << tree_level
        far = rows_whole(passed_along(offset, "tm", direction * distance), 0)
        has_peer = time_index >= distance if direction > 0 else time_index < devices - distance
        offset = jnp.where(has_peer, offset + matmul(lead, far), offset)
    return offset


def exit_levels(offset, leads, next_lead, direction, devices, time_index):
    for tree_level, lead in enumerate(leads[:-1]):
        distance = 1 << tree_level
        far = rows_whole(passed_along(offset, "tm", direction * distance), 0)
        has_peer = time_index >= distance if direction > 0 else time_index < devices - distance
        offset = jnp.where(has_peer, offset + matmul(lead, far), offset)
    distance = 1 << (len(leads) - 1)
    near = passed_along(offset, "tm", direction)
    far = rows_whole(passed_along(offset, "tm", direction * (distance + 1)), 0)
    neighbour = time_index - direction
    has_peer = neighbour >= distance if direction > 0 else neighbour < devices - distance
    return jnp.where(has_peer, near + matmul(next_lead, far), near)


def per_device(observed, gain, smooth_gain, dynamics, pattern, initial, lengths):
    steps_local, row_count, tracks = observed.shape
    devices = lax.axis_size("tm")
    time_index = lax.axis_index("tm")
    row_start = lax.axis_index("rows") * row_count
    transition = masked_dynamics(pattern, dynamics)
    transposed = transition.T
    state_width = transition.shape[0]
    live_slots = jnp.arange(steps_local, dtype=jnp.int32) < lengths[0]
    column_ids = jnp.arange(state_width, dtype=jnp.int32)
    row_ids = row_start + jnp.arange(row_count, dtype=jnp.int32)
    identity_rows = (column_ids[None, :] == row_ids[:, None]).astype(jnp.float32)
    start_whole = lax.all_gather(initial, "rows", axis=0, tiled=True)
    obs_whole = lax.all_gather(observed, "rows", axis=1, tiled=True)
    at_first = time_index == 0
    at_last = time_index == devices - 1

    prev_gain = passed_across(gain, 1)
    prev_live = jnp.arange(steps_local, dtype=jnp.int32) < passed_across(lengths, 1)[0]
    prev_lead, _ = lead_chain(
        identity_rows, 1.0 - prev_gain, prev_live, lambda x: matmul(x, transition), True
    )
    fwd_leads = lead_levels(jnp.where(at_first, 0.0, prev_lead), 1, devices, time_index)

    def from_zero(mean_whole, step_inputs):
        obs_now, rate_now, is_live = step_inputs
        fresh = (1.0 - rate_now)[:, None] * matmul(transition, mean_whole) + rate_now[:, None] * obs_now
        return jnp.where(is_live, fresh, mean_whole), None

    own_end, _ = lax.scan(
        from_zero, jnp.zeros((state_width, tracks), jnp.float32), (obs_whole, gain, live_slots),
        unroll=True,
    )
    prev_offset = passed_along(lax.dynamic_slice_in_dim(own_end, row_start, row_count, 0), "tm", 1)
    entry_rows = offset_levels(
        jnp.where(at_first, initial, prev_offset), fwd_leads, 1, devices, time_index
    )
    entry_whole = rows_whole(entry_rows, 0)

    back_lead, back_before = lead_chain(
        identity_rows, smooth_gain, live_slots, lambda x: matmul(x, transposed), False
    )
    back_leads = lead_levels(jnp.where(at_last, 0.0, back_lead), -1, devices, time_index)
    next_lead = passed_along(back_leads[-1], "tm", -1)

    def forward(mean_whole, step_inputs):
        obs_now, rate_now, is_live = step_inputs
        image_now = matmul(transition, mean_whole)
        fresh = (1.0 - rate_now)[:, None] * image_now + rate_now[:, None] * obs_now
        mean_next = jnp.where(is_live, fresh, mean_whole)
        return mean_next, (mean_next, image_now)

    final_mean, (filtered_whole, images) = lax.scan(
        forward, entry_whole, (obs_whole, gain, live_slots), unroll=True
    )
    terminal = matmul(transition, final_mean)
    image_all = jnp.concatenate([images[1:], terminal[None]], axis=0)
    pulled = jnp.einsum("ij,tjk->tik", transposed, image_all, precision=HIGHEST,
                        preferred_element_type=jnp.float32)
    offsets = filtered_whole - smooth_gain[:, :, None] * pulled

    live_offsets = jnp.where(live_slots[:, None, None], offsets, 0.0)
    back_offset = jnp.sum(batched(back_before, live_offsets), axis=0)
    back_offset = jnp.where(at_last, back_offset + matmul(back_lead, terminal), back_offset)
    next_inclusive = exit_levels(back_offset, back_leads, next_lead, -1, devices, time_index)
    terminal_rows = lax.dynamic_slice_in_dim(terminal, row_start, row_count, 0)
    after_rows = jnp.where(at_last, terminal_rows, next_inclusive)
    after_whole = rows_whole(after_rows, 0)

    def backward(later_whole, step_inputs):
        offset_now, keep_now, is_live = step_inputs
        fresh = keep_now[:, None] * matmul(transposed, later_whole) + offset_now
        smooth_now = jnp.where(is_live, fresh, later_whole)
        return smooth_now, smooth_now

    first_whole, smoothed_whole = lax.scan(
        backward, after_whole, (offsets, smooth_gain, live_slots), reverse=True, unroll=True
    )
    filtered = lax.dynamic_slice_in_dim(filtered_whole, row_start, row_count, 1)
    smoothed = lax.dynamic_slice_in_dim(smoothed_whole, row_start, row_count, 1)
    return (filtered, smoothed)


def solution(mesh):
    placed = (
        P("tm", "rows", None),
        P("tm", None),
        P("tm", None),
        P(),
        P(),
        P("rows", None),
        P("tm"),
    )
    return jax.shard_map(
        per_device,
        mesh=mesh,
        in_specs=placed,
        out_specs=(P("tm", "rows", None), P("tm", "rows", None)),
        check_vma=False,
    )
```

```python
import jax
import jax.numpy as jnp
from jax import lax
from jax.sharding import PartitionSpec as P

HIGHEST = lax.Precision.HIGHEST


def passed_along(block, axis, distance):
    devices = range(lax.axis_size(axis))
    route = [(i - distance, i) for i in devices if i - distance in devices]
    return lax.ppermute(block, axis, route)


def passed_across(block, distance):
    count, cores = lax.axis_size("tm"), lax.axis_size("rows")
    route = [
        ((i - distance) * cores + (cores - 1 - r), i * cores + r)
        for i in range(count)
        if 0 <= i - distance < count
        for r in range(cores)
    ]
    return lax.ppermute(block, ("tm", "rows"), route)


def rows_whole(part, axis):
    count = lax.axis_size("rows")
    if count != 2:
        return lax.all_gather(part, "rows", axis=axis, tiled=True)
    other = lax.ppermute(part, "rows", [(0, 1), (1, 0)])
    first_half = lax.axis_index("rows") == 0
    lower = jnp.where(first_half, part, other)
    upper = jnp.where(first_half, other, part)
    return jnp.concatenate([lower, upper], axis=axis)


def matmul(left, right):
    return jnp.dot(left, right, precision=HIGHEST, preferred_element_type=jnp.float32)


def left_transposed(left, right):
    return lax.dot_general(
        left, right, (((0,), (0,)), ((), ())), precision=HIGHEST, preferred_element_type=jnp.float32
    )


def right_transposed(left, right):
    return lax.dot_general(
        left, right, (((1,), (1,)), ((), ())), precision=HIGHEST, preferred_element_type=jnp.float32
    )


def batched(left, right):
    return lax.dot_general(
        left, right, (((2,), (1,)), ((0,), (0,))), precision=HIGHEST, preferred_element_type=jnp.float32
    )


def masked_dynamics(pattern, dynamics):
    blocks = pattern.shape[0]
    block_width = dynamics.shape[0] // blocks
    spread = jnp.broadcast_to(
        pattern.astype(dynamics.dtype)[:, None, :, None], (blocks, block_width, blocks, block_width)
    )
    return dynamics * spread.reshape(dynamics.shape)


def lead_chain(start_rows, scales, live_slots, apply, backwards):
    def advance(lead, step_inputs):
        scale, is_live = step_inputs
        fresh = apply(lead * scale[None, :])
        return jnp.where(is_live, fresh, lead), lead

    return lax.scan(advance, start_rows, (scales, live_slots), reverse=backwards, unroll=True)


def lead_levels(lead, direction, devices, time_index):
    levels = (devices - 1).bit_length()
    leads = [lead]
    for tree_level in range(levels - 1):
        distance = 1 << tree_level
        far = rows_whole(passed_along(leads[-1], "tm", direction * distance), 0)
        has_peer = time_index >= distance if direction > 0 else time_index < devices - distance
        leads.append(jnp.where(has_peer, matmul(leads[-1], far), leads[-1]))
    return leads[:levels]


def offset_levels(offset, leads, direction, devices, time_index):
    for tree_level, lead in enumerate(leads):
        distance = 1 << tree_level
        far = rows_whole(passed_along(offset, "tm", direction * distance), 0)
        has_peer = time_index >= distance if direction > 0 else time_index < devices - distance
        offset = jnp.where(has_peer, offset + matmul(lead, far), offset)
    return offset


def exit_levels(offset, leads, next_lead, direction, devices, time_index):
    for tree_level, lead in enumerate(leads[:-1]):
        distance = 1 << tree_level
        far = rows_whole(passed_along(offset, "tm", direction * distance), 0)
        has_peer = time_index >= distance if direction > 0 else time_index < devices - distance
        offset = jnp.where(has_peer, offset + matmul(lead, far), offset)
    distance = 1 << (len(leads) - 1)
    near = passed_along(offset, "tm", direction)
    far = rows_whole(passed_along(offset, "tm", direction * (distance + 1)), 0)
    neighbour = time_index - direction
    has_peer = neighbour >= distance if direction > 0 else neighbour < devices - distance
    return jnp.where(has_peer, near + matmul(next_lead, far), near)


def per_device(observed, gain, smooth_gain, dynamics, pattern, initial, lengths):
    steps_local, row_count, tracks = observed.shape
    devices = lax.axis_size("tm")
    time_index = lax.axis_index("tm")
    row_start = lax.axis_index("rows") * row_count
    transition = masked_dynamics(pattern, dynamics)
    transposed = transition.T
    state_width = transition.shape[0]
    live_slots = jnp.arange(steps_local, dtype=jnp.int32) < lengths[0]
    column_ids = jnp.arange(state_width, dtype=jnp.int32)
    row_ids = row_start + jnp.arange(row_count, dtype=jnp.int32)
    identity_rows = (column_ids[None, :] == row_ids[:, None]).astype(jnp.float32)
    start_whole = lax.all_gather(initial, "rows", axis=0, tiled=True)
    obs_whole = lax.all_gather(observed, "rows", axis=1, tiled=True)
    at_first = time_index == 0
    at_last = time_index == devices - 1

    prev_gain = passed_across(gain, 1)
    prev_live = jnp.arange(steps_local, dtype=jnp.int32) < passed_across(lengths, 1)[0]
    prev_lead, _ = lead_chain(
        identity_rows, 1.0 - prev_gain, prev_live, lambda x: matmul(x, transition), True
    )
    fwd_leads = lead_levels(jnp.where(at_first, 0.0, prev_lead), 1, devices, time_index)

    def from_zero(mean_whole, step_inputs):
        obs_now, rate_now, is_live = step_inputs
        fresh = (1.0 - rate_now)[:, None] * matmul(transition, mean_whole) + rate_now[:, None] * obs_now
        return jnp.where(is_live, fresh, mean_whole), None

    zero_start = jnp.zeros((state_width, tracks), jnp.float32) + 0.0 * prev_lead[:1, :1]
    own_end, _ = lax.scan(
        from_zero, zero_start, (obs_whole, gain, live_slots),
        unroll=True,
    )
    prev_offset = passed_along(lax.dynamic_slice_in_dim(own_end, row_start, row_count, 0), "tm", 1)
    entry_rows = offset_levels(
        jnp.where(at_first, initial, prev_offset), fwd_leads, 1, devices, time_index
    )
    entry_whole = rows_whole(entry_rows, 0)

    back_start = identity_rows + 0.0 * fwd_leads[min(1, len(fwd_leads) - 1)][:1, :1]
    back_lead, back_before = lead_chain(
        back_start, smooth_gain, live_slots, lambda x: matmul(x, transposed), False
    )
    back_leads = lead_levels(jnp.where(at_last, 0.0, back_lead), -1, devices, time_index)
    next_lead = passed_along(back_leads[-1], "tm", -1)

    def forward(mean_whole, step_inputs):
        obs_now, rate_now, is_live = step_inputs
        image_now = matmul(transition, mean_whole)
        fresh = (1.0 - rate_now)[:, None] * image_now + rate_now[:, None] * obs_now
        mean_next = jnp.where(is_live, fresh, mean_whole)
        return mean_next, (mean_next, image_now)

    final_mean, (filtered_whole, images) = lax.scan(
        forward, entry_whole, (obs_whole, gain, live_slots), unroll=True
    )
    terminal = matmul(transition, final_mean)
    image_all = jnp.concatenate([images[1:], terminal[None]], axis=0)
    pulled = jnp.einsum("ij,tjk->tik", transposed, image_all, precision=HIGHEST,
                        preferred_element_type=jnp.float32)
    offsets = filtered_whole - smooth_gain[:, :, None] * pulled

    live_offsets = jnp.where(live_slots[:, None, None], offsets, 0.0)
    back_offset = jnp.sum(batched(back_before, live_offsets), axis=0)
    back_offset = jnp.where(at_last, back_offset + matmul(back_lead, terminal), back_offset)
    next_inclusive = exit_levels(back_offset, back_leads, next_lead, -1, devices, time_index)
    terminal_rows = lax.dynamic_slice_in_dim(terminal, row_start, row_count, 0)
    after_rows = jnp.where(at_last, terminal_rows, next_inclusive)
    after_whole = rows_whole(after_rows, 0)

    def backward(later_whole, step_inputs):
        offset_now, keep_now, is_live = step_inputs
        fresh = keep_now[:, None] * matmul(transposed, later_whole) + offset_now
        smooth_now = jnp.where(is_live, fresh, later_whole)
        return smooth_now, smooth_now

    first_whole, smoothed_whole = lax.scan(
        backward, after_whole, (offsets, smooth_gain, live_slots), reverse=True, unroll=True
    )
    filtered = lax.dynamic_slice_in_dim(filtered_whole, row_start, row_count, 1)
    smoothed = lax.dynamic_slice_in_dim(smoothed_whole, row_start, row_count, 1)
    return (filtered, smoothed)


def solution(mesh):
    placed = (
        P("tm", "rows", None),
        P("tm", None),
        P("tm", None),
        P(),
        P(),
        P("rows", None),
        P("tm"),
    )
    return jax.shard_map(
        per_device,
        mesh=mesh,
        in_specs=placed,
        out_specs=(P("tm", "rows", None), P("tm", "rows", None)),
        check_vma=False,
    )
```

```python
import jax
import jax.numpy as jnp
from jax import lax
from jax.experimental.layout import Layout, with_layout_constraint
from jax.sharding import PartitionSpec as P

HIGHEST = lax.Precision.HIGHEST


def passed_along(block, axis, distance):
    devices = range(lax.axis_size(axis))
    route = [(i - distance, i) for i in devices if i - distance in devices]
    return lax.ppermute(block, axis, route)


def rows_whole(part, axis):
    count = lax.axis_size("rows")
    if count != 2:
        return lax.all_gather(part, "rows", axis=axis, tiled=True)
    other = lax.ppermute(part, "rows", [(0, 1), (1, 0)])
    first_half = lax.axis_index("rows") == 0
    lower = jnp.where(first_half, part, other)
    upper = jnp.where(first_half, other, part)
    return jnp.concatenate([lower, upper], axis=axis)


def matmul(left, right):
    return jnp.dot(left, right, precision=HIGHEST, preferred_element_type=jnp.float32)


def left_transposed(left, right):
    return lax.dot_general(
        left, right, (((0,), (0,)), ((), ())), precision=HIGHEST, preferred_element_type=jnp.float32
    )


def right_transposed(left, right):
    return lax.dot_general(
        left, right, (((1,), (1,)), ((), ())), precision=HIGHEST, preferred_element_type=jnp.float32
    )


def batched(left, right):
    return lax.dot_general(
        left, right, (((2,), (1,)), ((0,), (0,))), precision=HIGHEST, preferred_element_type=jnp.float32
    )


def masked_dynamics(pattern, dynamics):
    blocks = pattern.shape[0]
    block_width = dynamics.shape[0] // blocks
    spread = jnp.broadcast_to(
        pattern.astype(dynamics.dtype)[:, None, :, None], (blocks, block_width, blocks, block_width)
    )
    return dynamics * spread.reshape(dynamics.shape)


def lead_chain(start_rows, scales, live_slots, apply, backwards):
    def advance(lead, step_inputs):
        scale, is_live = step_inputs
        fresh = apply(lead * scale[None, :])
        return jnp.where(is_live, fresh, lead), lead

    return lax.scan(advance, start_rows, (scales, live_slots), reverse=backwards, unroll=True)


def lead_levels(lead, direction, devices, time_index):
    levels = (devices - 1).bit_length()
    leads = [lead]
    for tree_level in range(levels - 1):
        distance = 1 << tree_level
        far = rows_whole(passed_along(leads[-1], "tm", direction * distance), 0)
        has_peer = time_index >= distance if direction > 0 else time_index < devices - distance
        leads.append(jnp.where(has_peer, matmul(leads[-1], far), leads[-1]))
    return leads[:levels]


def offset_levels(offset, leads, direction, devices, time_index):
    for tree_level, lead in enumerate(leads):
        distance = 1 << tree_level
        far = rows_whole(passed_along(offset, "tm", direction * distance), 0)
        has_peer = time_index >= distance if direction > 0 else time_index < devices - distance
        offset = jnp.where(has_peer, offset + matmul(lead, far), offset)
    return offset


def per_device(observed, gain, smooth_gain, dynamics, pattern, initial, lengths):
    steps_local, row_count, tracks = observed.shape
    devices = lax.axis_size("tm")
    time_index = lax.axis_index("tm")
    row_start = lax.axis_index("rows") * row_count
    transition = masked_dynamics(pattern, dynamics)
    transposed = with_layout_constraint(transition.T, Layout(major_to_minor=(0, 1)))
    state_width = transition.shape[0]
    live_slots = jnp.arange(steps_local, dtype=jnp.int32) < lengths[0]
    column_ids = jnp.arange(state_width, dtype=jnp.int32)
    row_ids = row_start + jnp.arange(row_count, dtype=jnp.int32)
    identity_rows = (column_ids[None, :] == row_ids[:, None]).astype(jnp.float32)
    start_whole = lax.all_gather(initial, "rows", axis=0, tiled=True)
    obs_whole = lax.all_gather(observed, "rows", axis=1, tiled=True)
    at_first = time_index == 0
    at_last = time_index == devices - 1

    fwd_lead, fwd_before = lead_chain(
        identity_rows, 1.0 - gain, live_slots, lambda x: matmul(x, transition), True
    )
    fwd_leads = lead_levels(jnp.where(at_first, 0.0, fwd_lead), 1, devices, time_index)
    inputs = jnp.where(live_slots[:, None, None], gain[:, :, None] * obs_whole, 0.0)
    fwd_offset = jnp.sum(batched(fwd_before, inputs), axis=0)
    fwd_offset = jnp.where(at_first, fwd_offset + matmul(fwd_lead, start_whole), fwd_offset)
    fwd_inclusive = offset_levels(fwd_offset, fwd_leads, 1, devices, time_index)
    entry_rows = jnp.where(at_first, initial, passed_along(fwd_inclusive, "tm", 1))
    entry_whole = rows_whole(entry_rows, 0)

    back_lead, back_before = lead_chain(
        identity_rows, smooth_gain, live_slots, lambda x: matmul(x, transposed), False
    )
    back_leads = lead_levels(jnp.where(at_last, 0.0, back_lead), -1, devices, time_index)

    def forward(mean_whole, step_inputs):
        obs_now, rate_now, is_live = step_inputs
        image_now = matmul(transition, mean_whole)
        fresh = (1.0 - rate_now)[:, None] * image_now + rate_now[:, None] * obs_now
        mean_next = jnp.where(is_live, fresh, mean_whole)
        return mean_next, (mean_next, image_now)

    final_mean, (filtered_whole, images) = lax.scan(
        forward, entry_whole, (obs_whole, gain, live_slots), unroll=True
    )
    terminal = matmul(transition, final_mean)
    image_all = jnp.concatenate([images[1:], terminal[None]], axis=0)
    pulled = jnp.einsum("ij,tjk->tik", transposed, image_all, precision=HIGHEST,
                        preferred_element_type=jnp.float32)
    offsets = filtered_whole - smooth_gain[:, :, None] * pulled

    live_offsets = jnp.where(live_slots[:, None, None], offsets, 0.0)
    back_offset = jnp.sum(batched(back_before, live_offsets), axis=0)
    back_offset = jnp.where(at_last, back_offset + matmul(back_lead, terminal), back_offset)
    back_inclusive = offset_levels(back_offset, back_leads, -1, devices, time_index)
    terminal_rows = lax.dynamic_slice_in_dim(terminal, row_start, row_count, 0)
    after_rows = jnp.where(at_last, terminal_rows, passed_along(back_inclusive, "tm", -1))
    after_whole = rows_whole(after_rows, 0)

    def backward(later_whole, step_inputs):
        offset_now, keep_now, is_live = step_inputs
        fresh = keep_now[:, None] * matmul(transposed, later_whole) + offset_now
        smooth_now = jnp.where(is_live, fresh, later_whole)
        return smooth_now, smooth_now

    first_whole, smoothed_whole = lax.scan(
        backward, after_whole, (offsets, smooth_gain, live_slots), reverse=True, unroll=True
    )
    filtered = lax.dynamic_slice_in_dim(filtered_whole, row_start, row_count, 1)
    smoothed = lax.dynamic_slice_in_dim(smoothed_whole, row_start, row_count, 1)
    return (filtered, smoothed)


def solution(mesh):
    placed = (
        P("tm", "rows", None),
        P("tm", None),
        P("tm", None),
        P(),
        P(),
        P("rows", None),
        P("tm"),
    )
    return jax.shard_map(
        per_device,
        mesh=mesh,
        in_specs=placed,
        out_specs=(P("tm", "rows", None), P("tm", "rows", None)),
        check_vma=False,
    )
```

```python
import jax
import jax.numpy as jnp
from jax import lax
from jax.experimental.layout import Layout, with_layout_constraint
from jax.sharding import PartitionSpec as P

HIGHEST = lax.Precision.HIGHEST


def passed_along(block, axis, distance):
    devices = range(lax.axis_size(axis))
    route = [(i - distance, i) for i in devices if i - distance in devices]
    return lax.ppermute(block, axis, route)


def rows_whole(part, axis):
    count = lax.axis_size("rows")
    if count != 2:
        return lax.all_gather(part, "rows", axis=axis, tiled=True)
    other = lax.ppermute(part, "rows", [(0, 1), (1, 0)])
    first_half = lax.axis_index("rows") == 0
    lower = jnp.where(first_half, part, other)
    upper = jnp.where(first_half, other, part)
    return jnp.concatenate([lower, upper], axis=axis)


def matmul(left, right):
    return jnp.dot(left, right, precision=HIGHEST, preferred_element_type=jnp.float32)


def left_transposed(left, right):
    return lax.dot_general(
        left, right, (((0,), (0,)), ((), ())), precision=HIGHEST, preferred_element_type=jnp.float32
    )


def right_transposed(left, right):
    return lax.dot_general(
        left, right, (((1,), (1,)), ((), ())), precision=HIGHEST, preferred_element_type=jnp.float32
    )


def batched(left, right):
    return lax.dot_general(
        left, right, (((2,), (1,)), ((0,), (0,))), precision=HIGHEST, preferred_element_type=jnp.float32
    )


def masked_dynamics(pattern, dynamics):
    blocks = pattern.shape[0]
    block_width = dynamics.shape[0] // blocks
    spread = jnp.broadcast_to(
        pattern.astype(dynamics.dtype)[:, None, :, None], (blocks, block_width, blocks, block_width)
    )
    return dynamics * spread.reshape(dynamics.shape)


def lead_chain(start_rows, scales, live_slots, apply, backwards):
    def advance(lead, step_inputs):
        scale, is_live = step_inputs
        fresh = apply(lead * scale[None, :])
        return jnp.where(is_live, fresh, lead), lead

    return lax.scan(advance, start_rows, (scales, live_slots), reverse=backwards, unroll=True)


def lead_levels(lead, direction, devices, time_index):
    levels = (devices - 1).bit_length()
    leads = [lead]
    for tree_level in range(levels - 1):
        distance = 1 << tree_level
        far = rows_whole(passed_along(leads[-1], "tm", direction * distance), 0)
        has_peer = time_index >= distance if direction > 0 else time_index < devices - distance
        leads.append(jnp.where(has_peer, matmul(leads[-1], far), leads[-1]))
    return leads[:levels]


def offset_levels(offset, leads, direction, devices, time_index):
    for tree_level, lead in enumerate(leads):
        distance = 1 << tree_level
        far = rows_whole(passed_along(offset, "tm", direction * distance), 0)
        has_peer = time_index >= distance if direction > 0 else time_index < devices - distance
        offset = jnp.where(has_peer, offset + matmul(lead, far), offset)
    return offset


def per_device(observed, gain, smooth_gain, dynamics, pattern, initial, lengths):
    steps_local, row_count, tracks = observed.shape
    devices = lax.axis_size("tm")
    time_index = lax.axis_index("tm")
    row_start = lax.axis_index("rows") * row_count
    transition = masked_dynamics(pattern, dynamics)
    transposed = with_layout_constraint(transition.T, Layout(major_to_minor=(0, 1)))
    state_width = transition.shape[0]
    live_slots = jnp.arange(steps_local, dtype=jnp.int32) < lengths[0]
    column_ids = jnp.arange(state_width, dtype=jnp.int32)
    row_ids = row_start + jnp.arange(row_count, dtype=jnp.int32)
    identity_rows = (column_ids[None, :] == row_ids[:, None]).astype(jnp.float32)
    start_whole = lax.all_gather(initial, "rows", axis=0, tiled=True)
    obs_whole = lax.all_gather(observed, "rows", axis=1, tiled=True)
    at_first = time_index == 0
    at_last = time_index == devices - 1

    fwd_lead, fwd_before = lead_chain(
        identity_rows, 1.0 - gain, live_slots, lambda x: matmul(x, transition), True
    )
    fwd_leads = lead_levels(jnp.where(at_first, 0.0, fwd_lead), 1, devices, time_index)
    inputs = jnp.where(live_slots[:, None, None], gain[:, :, None] * obs_whole, 0.0)
    fwd_offset = jnp.sum(batched(fwd_before, inputs), axis=0)
    fwd_offset = jnp.where(at_first, fwd_offset + matmul(fwd_lead, start_whole), fwd_offset)
    fwd_inclusive = offset_levels(fwd_offset, fwd_leads, 1, devices, time_index)
    entry_rows = jnp.where(at_first, initial, passed_along(fwd_inclusive, "tm", 1))
    entry_whole = rows_whole(entry_rows, 0)

    back_lead, back_before = lead_chain(
        identity_rows, smooth_gain, live_slots, lambda x: right_transposed(x, transition), False
    )
    back_leads = lead_levels(jnp.where(at_last, 0.0, back_lead), -1, devices, time_index)

    def forward(mean_whole, step_inputs):
        obs_now, rate_now, is_live = step_inputs
        image_now = matmul(transition, mean_whole)
        fresh = (1.0 - rate_now)[:, None] * image_now + rate_now[:, None] * obs_now
        mean_next = jnp.where(is_live, fresh, mean_whole)
        return mean_next, (mean_next, image_now)

    final_mean, (filtered_whole, images) = lax.scan(
        forward, entry_whole, (obs_whole, gain, live_slots), unroll=True
    )
    terminal = matmul(transition, final_mean)
    image_all = jnp.concatenate([images[1:], terminal[None]], axis=0)
    pulled = jnp.einsum("ji,tjk->tik", transition, image_all, precision=HIGHEST,
                        preferred_element_type=jnp.float32)
    offsets = filtered_whole - smooth_gain[:, :, None] * pulled

    live_offsets = jnp.where(live_slots[:, None, None], offsets, 0.0)
    back_offset = jnp.sum(batched(back_before, live_offsets), axis=0)
    back_offset = jnp.where(at_last, back_offset + matmul(back_lead, terminal), back_offset)
    back_inclusive = offset_levels(back_offset, back_leads, -1, devices, time_index)
    terminal_rows = lax.dynamic_slice_in_dim(terminal, row_start, row_count, 0)
    after_rows = jnp.where(at_last, terminal_rows, passed_along(back_inclusive, "tm", -1))
    after_whole = rows_whole(after_rows, 0)

    def backward(later_whole, step_inputs):
        offset_now, keep_now, is_live = step_inputs
        fresh = keep_now[:, None] * matmul(transposed, later_whole) + offset_now
        smooth_now = jnp.where(is_live, fresh, later_whole)
        return smooth_now, smooth_now

    first_whole, smoothed_whole = lax.scan(
        backward, after_whole, (offsets, smooth_gain, live_slots), reverse=True, unroll=True
    )
    filtered = lax.dynamic_slice_in_dim(filtered_whole, row_start, row_count, 1)
    smoothed = lax.dynamic_slice_in_dim(smoothed_whole, row_start, row_count, 1)
    return (filtered, smoothed)


def solution(mesh):
    placed = (
        P("tm", "rows", None),
        P("tm", None),
        P("tm", None),
        P(),
        P(),
        P("rows", None),
        P("tm"),
    )
    return jax.shard_map(
        per_device,
        mesh=mesh,
        in_specs=placed,
        out_specs=(P("tm", "rows", None), P("tm", "rows", None)),
        check_vma=False,
    )
```

```python
import jax
import jax.numpy as jnp
from jax import lax
from jax.experimental.layout import Layout, with_layout_constraint
from jax.sharding import PartitionSpec as P

HIGHEST = lax.Precision.HIGHEST


def passed_along(block, axis, distance):
    devices = range(lax.axis_size(axis))
    route = [(i - distance, i) for i in devices if i - distance in devices]
    return lax.ppermute(block, axis, route)


def rows_whole(part, axis):
    count = lax.axis_size("rows")
    if count != 2:
        return lax.all_gather(part, "rows", axis=axis, tiled=True)
    other = lax.ppermute(part, "rows", [(0, 1), (1, 0)])
    first_half = lax.axis_index("rows") == 0
    lower = jnp.where(first_half, part, other)
    upper = jnp.where(first_half, other, part)
    return jnp.concatenate([lower, upper], axis=axis)


def matmul(left, right):
    return jnp.dot(left, right, precision=HIGHEST, preferred_element_type=jnp.float32)


def left_transposed(left, right):
    return lax.dot_general(
        left, right, (((0,), (0,)), ((), ())), precision=HIGHEST, preferred_element_type=jnp.float32
    )


def right_transposed(left, right):
    return lax.dot_general(
        left, right, (((1,), (1,)), ((), ())), precision=HIGHEST, preferred_element_type=jnp.float32
    )


def batched(left, right):
    return lax.dot_general(
        left, right, (((2,), (1,)), ((0,), (0,))), precision=HIGHEST, preferred_element_type=jnp.float32
    )


def masked_dynamics(pattern, dynamics):
    blocks = pattern.shape[0]
    block_width = dynamics.shape[0] // blocks
    spread = jnp.broadcast_to(
        pattern.astype(dynamics.dtype)[:, None, :, None], (blocks, block_width, blocks, block_width)
    )
    return dynamics * spread.reshape(dynamics.shape)


def lead_chain(start_rows, scales, live_slots, apply, backwards):
    def advance(lead, step_inputs):
        scale, is_live = step_inputs
        fresh = apply(lead * scale[None, :])
        return jnp.where(is_live, fresh, lead), lead

    return lax.scan(advance, start_rows, (scales, live_slots), reverse=backwards, unroll=True)


def lead_levels(lead, direction, devices, time_index):
    levels = (devices - 1).bit_length()
    leads = [lead]
    for tree_level in range(levels - 1):
        distance = 1 << tree_level
        far = rows_whole(passed_along(leads[-1], "tm", direction * distance), 0)
        has_peer = time_index >= distance if direction > 0 else time_index < devices - distance
        leads.append(jnp.where(has_peer, matmul(leads[-1], far), leads[-1]))
    return leads[:levels]


def offset_levels(offset, leads, direction, devices, time_index):
    for tree_level, lead in enumerate(leads):
        distance = 1 << tree_level
        far = rows_whole(passed_along(offset, "tm", direction * distance), 0)
        has_peer = time_index >= distance if direction > 0 else time_index < devices - distance
        offset = jnp.where(has_peer, offset + matmul(lead, far), offset)
    return offset


def per_device(observed, gain, smooth_gain, dynamics, pattern, initial, lengths):
    steps_local, row_count, tracks = observed.shape
    devices = lax.axis_size("tm")
    time_index = lax.axis_index("tm")
    row_start = lax.axis_index("rows") * row_count
    row_major = Layout(major_to_minor=(0, 1))
    transition = with_layout_constraint(masked_dynamics(pattern, dynamics), row_major)
    transposed = with_layout_constraint(transition.T, row_major)
    state_width = transition.shape[0]
    live_slots = jnp.arange(steps_local, dtype=jnp.int32) < lengths[0]
    column_ids = jnp.arange(state_width, dtype=jnp.int32)
    row_ids = row_start + jnp.arange(row_count, dtype=jnp.int32)
    identity_rows = (column_ids[None, :] == row_ids[:, None]).astype(jnp.float32)
    start_whole = lax.all_gather(initial, "rows", axis=0, tiled=True)
    obs_whole = lax.all_gather(observed, "rows", axis=1, tiled=True)
    at_first = time_index == 0
    at_last = time_index == devices - 1

    fwd_lead, fwd_before = lead_chain(
        identity_rows, 1.0 - gain, live_slots, lambda x: matmul(x, transition), True
    )
    fwd_leads = lead_levels(jnp.where(at_first, 0.0, fwd_lead), 1, devices, time_index)
    inputs = jnp.where(live_slots[:, None, None], gain[:, :, None] * obs_whole, 0.0)
    fwd_offset = jnp.sum(batched(fwd_before, inputs), axis=0)
    fwd_offset = jnp.where(at_first, fwd_offset + matmul(fwd_lead, start_whole), fwd_offset)
    fwd_inclusive = offset_levels(fwd_offset, fwd_leads, 1, devices, time_index)
    entry_rows = jnp.where(at_first, initial, passed_along(fwd_inclusive, "tm", 1))
    entry_whole = rows_whole(entry_rows, 0)

    back_lead, back_before = lead_chain(
        identity_rows, smooth_gain, live_slots, lambda x: right_transposed(x, transition), False
    )
    back_leads = lead_levels(jnp.where(at_last, 0.0, back_lead), -1, devices, time_index)

    def forward(mean_whole, step_inputs):
        obs_now, rate_now, is_live = step_inputs
        image_now = matmul(transition, mean_whole)
        fresh = (1.0 - rate_now)[:, None] * image_now + rate_now[:, None] * obs_now
        mean_next = jnp.where(is_live, fresh, mean_whole)
        return mean_next, (mean_next, image_now)

    final_mean, (filtered_whole, images) = lax.scan(
        forward, entry_whole, (obs_whole, gain, live_slots), unroll=True
    )
    terminal = matmul(transition, final_mean)
    image_all = jnp.concatenate([images[1:], terminal[None]], axis=0)
    pulled = jnp.einsum("ji,tjk->tik", transition, image_all, precision=HIGHEST,
                        preferred_element_type=jnp.float32)
    offsets = filtered_whole - smooth_gain[:, :, None] * pulled

    live_offsets = jnp.where(live_slots[:, None, None], offsets, 0.0)
    back_offset = jnp.sum(batched(back_before, live_offsets), axis=0)
    back_offset = jnp.where(at_last, back_offset + matmul(back_lead, terminal), back_offset)
    back_inclusive = offset_levels(back_offset, back_leads, -1, devices, time_index)
    terminal_rows = lax.dynamic_slice_in_dim(terminal, row_start, row_count, 0)
    after_rows = jnp.where(at_last, terminal_rows, passed_along(back_inclusive, "tm", -1))
    after_whole = rows_whole(after_rows, 0)

    def backward(later_whole, step_inputs):
        offset_now, keep_now, is_live = step_inputs
        fresh = keep_now[:, None] * matmul(transposed, later_whole) + offset_now
        smooth_now = jnp.where(is_live, fresh, later_whole)
        return smooth_now, smooth_now

    first_whole, smoothed_whole = lax.scan(
        backward, after_whole, (offsets, smooth_gain, live_slots), reverse=True, unroll=True
    )
    filtered = lax.dynamic_slice_in_dim(filtered_whole, row_start, row_count, 1)
    smoothed = lax.dynamic_slice_in_dim(smoothed_whole, row_start, row_count, 1)
    return (filtered, smoothed)


def solution(mesh):
    placed = (
        P("tm", "rows", None),
        P("tm", None),
        P("tm", None),
        P(),
        P(),
        P("rows", None),
        P("tm"),
    )
    return jax.shard_map(
        per_device,
        mesh=mesh,
        in_specs=placed,
        out_specs=(P("tm", "rows", None), P("tm", "rows", None)),
        check_vma=False,
    )
```

```python
import jax
import jax.numpy as jnp
from jax import lax
from jax.experimental.layout import Layout, with_layout_constraint
from jax.sharding import PartitionSpec as P

HIGHEST = lax.Precision.HIGHEST


def passed_along(block, axis, distance):
    devices = range(lax.axis_size(axis))
    route = [(i - distance, i) for i in devices if i - distance in devices]
    return lax.ppermute(block, axis, route)


def rows_whole(part, axis):
    count = lax.axis_size("rows")
    if count != 2:
        return lax.all_gather(part, "rows", axis=axis, tiled=True)
    other = lax.ppermute(part, "rows", [(0, 1), (1, 0)])
    first_half = lax.axis_index("rows") == 0
    lower = jnp.where(first_half, part, other)
    upper = jnp.where(first_half, other, part)
    return jnp.concatenate([lower, upper], axis=axis)


def matmul(left, right):
    return jnp.dot(left, right, precision=HIGHEST, preferred_element_type=jnp.float32)


def left_transposed(left, right):
    return lax.dot_general(
        left, right, (((0,), (0,)), ((), ())), precision=HIGHEST, preferred_element_type=jnp.float32
    )


def right_transposed(left, right):
    return lax.dot_general(
        left, right, (((1,), (1,)), ((), ())), precision=HIGHEST, preferred_element_type=jnp.float32
    )


def batched(left, right):
    return lax.dot_general(
        left, right, (((2,), (1,)), ((0,), (0,))), precision=HIGHEST, preferred_element_type=jnp.float32
    )


def masked_dynamics(pattern, dynamics):
    blocks = pattern.shape[0]
    block_width = dynamics.shape[0] // blocks
    spread = jnp.broadcast_to(
        pattern.astype(dynamics.dtype)[:, None, :, None], (blocks, block_width, blocks, block_width)
    )
    return dynamics * spread.reshape(dynamics.shape)


def lead_chain(start_rows, scales, live_slots, apply, backwards):
    def advance(lead, step_inputs):
        scale, is_live = step_inputs
        fresh = apply(lead * scale[None, :])
        return jnp.where(is_live, fresh, lead), lead

    return lax.scan(advance, start_rows, (scales, live_slots), reverse=backwards, unroll=True)


def lead_levels(lead, direction, devices, time_index):
    levels = (devices - 1).bit_length()
    leads = [lead]
    for tree_level in range(levels - 1):
        distance = 1 << tree_level
        far = rows_whole(passed_along(leads[-1], "tm", direction * distance), 0)
        has_peer = time_index >= distance if direction > 0 else time_index < devices - distance
        leads.append(jnp.where(has_peer, matmul(leads[-1], far), leads[-1]))
    return leads[:levels]


def offset_levels(offset, leads, direction, devices, time_index):
    for tree_level, lead in enumerate(leads):
        distance = 1 << tree_level
        far = rows_whole(passed_along(offset, "tm", direction * distance), 0)
        has_peer = time_index >= distance if direction > 0 else time_index < devices - distance
        offset = jnp.where(has_peer, offset + matmul(lead, far), offset)
    return offset


def per_device(observed, gain, smooth_gain, dynamics, pattern, initial, lengths):
    steps_local, row_count, tracks = observed.shape
    devices = lax.axis_size("tm")
    time_index = lax.axis_index("tm")
    row_start = lax.axis_index("rows") * row_count
    row_major = Layout(major_to_minor=(0, 1))
    transition = with_layout_constraint(masked_dynamics(pattern, dynamics), row_major)
    transposed = with_layout_constraint(transition.T, row_major)
    state_width = transition.shape[0]
    live_slots = jnp.arange(steps_local, dtype=jnp.int32) < lengths[0]
    column_ids = jnp.arange(state_width, dtype=jnp.int32)
    row_ids = row_start + jnp.arange(row_count, dtype=jnp.int32)
    identity_rows = (column_ids[None, :] == row_ids[:, None]).astype(jnp.float32)
    start_whole = lax.all_gather(initial, "rows", axis=0, tiled=True)
    obs_whole = lax.all_gather(observed, "rows", axis=1, tiled=True)
    at_first = time_index == 0
    at_last = time_index == devices - 1

    fwd_lead, fwd_before = lead_chain(
        identity_rows, 1.0 - gain, live_slots, lambda x: matmul(x, transition), True
    )
    fwd_leads = lead_levels(jnp.where(at_first, 0.0, fwd_lead), 1, devices, time_index)
    inputs = jnp.where(live_slots[:, None, None], gain[:, :, None] * obs_whole, 0.0)
    fwd_offset = jnp.sum(batched(fwd_before, inputs), axis=0)
    fwd_offset = jnp.where(at_first, fwd_offset + matmul(fwd_lead, start_whole), fwd_offset)
    fwd_inclusive = offset_levels(fwd_offset, fwd_leads, 1, devices, time_index)
    entry_rows = jnp.where(at_first, initial, passed_along(fwd_inclusive, "tm", 1))
    entry_whole = rows_whole(entry_rows, 0)

    back_lead, back_before = lead_chain(
        identity_rows, smooth_gain, live_slots, lambda x: matmul(x, transposed), False
    )
    back_leads = lead_levels(jnp.where(at_last, 0.0, back_lead), -1, devices, time_index)

    def forward(mean_whole, step_inputs):
        obs_now, rate_now, is_live = step_inputs
        image_now = matmul(transition, mean_whole)
        fresh = (1.0 - rate_now)[:, None] * image_now + rate_now[:, None] * obs_now
        mean_next = jnp.where(is_live, fresh, mean_whole)
        return mean_next, (mean_next, image_now)

    final_mean, (filtered_whole, images) = lax.scan(
        forward, entry_whole, (obs_whole, gain, live_slots), unroll=True
    )
    terminal = matmul(transition, final_mean)
    image_all = jnp.concatenate([images[1:], terminal[None]], axis=0)
    pulled = jnp.einsum("ij,tjk->tik", transposed, image_all, precision=HIGHEST,
                        preferred_element_type=jnp.float32)
    offsets = filtered_whole - smooth_gain[:, :, None] * pulled

    live_offsets = jnp.where(live_slots[:, None, None], offsets, 0.0)
    back_offset = jnp.sum(batched(back_before, live_offsets), axis=0)
    back_offset = jnp.where(at_last, back_offset + matmul(back_lead, terminal), back_offset)
    back_inclusive = offset_levels(back_offset, back_leads, -1, devices, time_index)
    terminal_rows = lax.dynamic_slice_in_dim(terminal, row_start, row_count, 0)
    after_rows = jnp.where(at_last, terminal_rows, passed_along(back_inclusive, "tm", -1))
    after_whole = rows_whole(after_rows, 0)

    def backward(later_whole, step_inputs):
        offset_now, keep_now, is_live = step_inputs
        fresh = keep_now[:, None] * matmul(transposed, later_whole) + offset_now
        smooth_now = jnp.where(is_live, fresh, later_whole)
        return smooth_now, smooth_now

    first_whole, smoothed_whole = lax.scan(
        backward, after_whole, (offsets, smooth_gain, live_slots), reverse=True, unroll=True
    )
    filtered = lax.dynamic_slice_in_dim(filtered_whole, row_start, row_count, 1)
    smoothed = lax.dynamic_slice_in_dim(smoothed_whole, row_start, row_count, 1)
    return (filtered, smoothed)


def solution(mesh):
    placed = (
        P("tm", "rows", None),
        P("tm", None),
        P("tm", None),
        P(),
        P(),
        P("rows", None),
        P("tm"),
    )
    return jax.shard_map(
        per_device,
        mesh=mesh,
        in_specs=placed,
        out_specs=(P("tm", "rows", None), P("tm", "rows", None)),
        check_vma=False,
    )
```

```python
import jax
import jax.numpy as jnp
from jax import lax
from jax.sharding import PartitionSpec as P

HIGHEST = lax.Precision.HIGHEST


def passed_along(block, axis, distance):
    devices = range(lax.axis_size(axis))
    route = [(i - distance, i) for i in devices if i - distance in devices]
    return lax.ppermute(block, axis, route)


def rows_whole(part, axis):
    count = lax.axis_size("rows")
    if count != 2:
        return lax.all_gather(part, "rows", axis=axis, tiled=True)
    other = lax.ppermute(part, "rows", [(0, 1), (1, 0)])
    first_half = lax.axis_index("rows") == 0
    lower = jnp.where(first_half, part, other)
    upper = jnp.where(first_half, other, part)
    return jnp.concatenate([lower, upper], axis=axis)


def matmul(left, right):
    return jnp.dot(left, right, precision=HIGHEST, preferred_element_type=jnp.float32)


def left_transposed(left, right):
    return lax.dot_general(
        left, right, (((0,), (0,)), ((), ())), precision=HIGHEST, preferred_element_type=jnp.float32
    )


def right_transposed(left, right):
    return lax.dot_general(
        left, right, (((1,), (1,)), ((), ())), precision=HIGHEST, preferred_element_type=jnp.float32
    )


def batched(left, right):
    return lax.dot_general(
        left, right, (((2,), (1,)), ((0,), (0,))), precision=HIGHEST, preferred_element_type=jnp.float32
    )


def masked_dynamics(pattern, dynamics):
    blocks = pattern.shape[0]
    block_width = dynamics.shape[0] // blocks
    spread = jnp.broadcast_to(
        pattern.astype(dynamics.dtype)[:, None, :, None], (blocks, block_width, blocks, block_width)
    )
    return dynamics * spread.reshape(dynamics.shape)


def lead_chain(start_rows, scales, live_slots, apply, backwards):
    def advance(lead, step_inputs):
        scale, is_live = step_inputs
        fresh = apply(lead * scale[None, :])
        return jnp.where(is_live, fresh, lead), lead

    return lax.scan(advance, start_rows, (scales, live_slots), reverse=backwards, unroll=True)


def lead_levels(lead, direction, devices, time_index):
    levels = (devices - 1).bit_length()
    leads = [lead]
    for tree_level in range(levels - 1):
        distance = 1 << tree_level
        far = rows_whole(passed_along(leads[-1], "tm", direction * distance), 0)
        has_peer = time_index >= distance if direction > 0 else time_index < devices - distance
        leads.append(jnp.where(has_peer, matmul(leads[-1], far), leads[-1]))
    return leads[:levels]


def offset_levels(offset, leads, direction, devices, time_index):
    for tree_level, lead in enumerate(leads):
        distance = 1 << tree_level
        far = rows_whole(passed_along(offset, "tm", direction * distance), 0)
        has_peer = time_index >= distance if direction > 0 else time_index < devices - distance
        offset = jnp.where(has_peer, offset + matmul(lead, far), offset)
    return offset


def exit_levels(offset, leads, next_lead, direction, devices, time_index):
    for tree_level, lead in enumerate(leads[:-1]):
        distance = 1 << tree_level
        far = rows_whole(passed_along(offset, "tm", direction * distance), 0)
        has_peer = time_index >= distance if direction > 0 else time_index < devices - distance
        offset = jnp.where(has_peer, offset + matmul(lead, far), offset)
    distance = 1 << (len(leads) - 1)
    near = passed_along(offset, "tm", direction)
    far = rows_whole(passed_along(offset, "tm", direction * (distance + 1)), 0)
    neighbour = time_index - direction
    has_peer = neighbour >= distance if direction > 0 else neighbour < devices - distance
    return jnp.where(has_peer, near + matmul(next_lead, far), near)


def per_device(observed, gain, smooth_gain, dynamics, pattern, initial, lengths):
    steps_local, row_count, tracks = observed.shape
    devices = lax.axis_size("tm")
    time_index = lax.axis_index("tm")
    row_start = lax.axis_index("rows") * row_count
    transition = masked_dynamics(pattern, dynamics)
    state_width = transition.shape[0]
    live_slots = jnp.arange(steps_local, dtype=jnp.int32) < lengths[0]
    column_ids = jnp.arange(state_width, dtype=jnp.int32)
    row_ids = row_start + jnp.arange(row_count, dtype=jnp.int32)
    identity_rows = (column_ids[None, :] == row_ids[:, None]).astype(jnp.float32)
    start_whole = lax.all_gather(initial, "rows", axis=0, tiled=True)
    obs_whole = lax.all_gather(observed, "rows", axis=1, tiled=True)
    at_first = time_index == 0
    at_last = time_index == devices - 1

    fwd_lead, fwd_before = lead_chain(
        identity_rows, 1.0 - gain, live_slots, lambda x: matmul(x, transition), True
    )
    fwd_leads = lead_levels(jnp.where(at_first, 0.0, fwd_lead), 1, devices, time_index)
    inputs = jnp.where(live_slots[:, None, None], gain[:, :, None] * obs_whole, 0.0)
    fwd_offset = jnp.sum(batched(fwd_before, inputs), axis=0)
    fwd_offset = jnp.where(at_first, fwd_offset + matmul(fwd_lead, start_whole), fwd_offset)
    fwd_inclusive = offset_levels(fwd_offset, fwd_leads, 1, devices, time_index)
    entry_rows = jnp.where(at_first, initial, passed_along(fwd_inclusive, "tm", 1))
    entry_whole = rows_whole(entry_rows, 0)

    back_lead, back_before = lead_chain(
        identity_rows, smooth_gain, live_slots, lambda x: right_transposed(x, transition), False
    )
    back_leads = lead_levels(jnp.where(at_last, 0.0, back_lead), -1, devices, time_index)
    next_lead = passed_along(back_leads[-1], "tm", -1)

    def forward(mean_whole, step_inputs):
        obs_now, rate_now, is_live = step_inputs
        image_now = matmul(transition, mean_whole)
        fresh = (1.0 - rate_now)[:, None] * image_now + rate_now[:, None] * obs_now
        mean_next = jnp.where(is_live, fresh, mean_whole)
        return mean_next, (mean_next, image_now)

    final_mean, (filtered_whole, images) = lax.scan(
        forward, entry_whole, (obs_whole, gain, live_slots), unroll=True
    )
    terminal = matmul(transition, final_mean)
    image_all = jnp.concatenate([images[1:], terminal[None]], axis=0)
    pulled = jnp.einsum("ji,tjk->tik", transition, image_all, precision=HIGHEST,
                        preferred_element_type=jnp.float32)
    offsets = filtered_whole - smooth_gain[:, :, None] * pulled

    live_offsets = jnp.where(live_slots[:, None, None], offsets, 0.0)
    back_offset = jnp.sum(batched(back_before, live_offsets), axis=0)
    back_offset = jnp.where(at_last, back_offset + matmul(back_lead, terminal), back_offset)
    next_inclusive = exit_levels(back_offset, back_leads, next_lead, -1, devices, time_index)
    terminal_rows = lax.dynamic_slice_in_dim(terminal, row_start, row_count, 0)
    after_rows = jnp.where(at_last, terminal_rows, next_inclusive)
    after_whole = rows_whole(after_rows, 0)

    def backward(later_whole, step_inputs):
        offset_now, keep_now, is_live = step_inputs
        fresh = keep_now[:, None] * left_transposed(transition, later_whole) + offset_now
        smooth_now = jnp.where(is_live, fresh, later_whole)
        return smooth_now, smooth_now

    first_whole, smoothed_whole = lax.scan(
        backward, after_whole, (offsets, smooth_gain, live_slots), reverse=True, unroll=True
    )
    filtered = lax.dynamic_slice_in_dim(filtered_whole, row_start, row_count, 1)
    smoothed = lax.dynamic_slice_in_dim(smoothed_whole, row_start, row_count, 1)
    return (filtered, smoothed)


def solution(mesh):
    placed = (
        P("tm", "rows", None),
        P("tm", None),
        P("tm", None),
        P(),
        P(),
        P("rows", None),
        P("tm"),
    )
    return jax.shard_map(
        per_device,
        mesh=mesh,
        in_specs=placed,
        out_specs=(P("tm", "rows", None), P("tm", "rows", None)),
        check_vma=False,
    )
```
